32 devices in a mesh: slab: 2 (over y), wide: 4 (over z), narrow: 2 (over x), inner: 2 (over core).
Axes of the slice: x: 2, y: 2, z: 4, core: 2. Of those that a mesh axis runs over, the one named last changes fastest.
Arguments:
- templates: bfloat16 [16384, 1024], P(('slab', 'wide', 'narrow', 'inner')), parts along dimension 0, may hold values from -6 to 6
- leaf_inverse: bfloat16 [16384, 512], P(('slab', 'wide', 'narrow', 'inner')), parts along dimension 0, may hold values from -0.25 to 0.25
- v_basis: bfloat16 [4, 16384, 128], P(None, ('slab', 'wide', 'narrow', 'inner')), parts along dimension 1, may hold values from -0.09375 to 0.09375
- u_basis: bfloat16 [4, 16384, 128], P(None, ('slab', 'wide', 'narrow', 'inner')), parts along dimension 1, may hold values from -0.5 to 0.5
- coupling: bfloat16 [4, 32, 128, 256], P(None, ('slab', 'wide', 'narrow', 'inner')), parts along dimension 1, may hold values from -1 to 1, as said below
Outputs:
- filtered: bfloat16 [16384, 1024], P(('slab', 'wide', 'narrow', 'inner')), parts along dimension 0
The draws below stay inside these ranges and needn't reach their ends.
There are 2 independent parts, one for each index of `slab`. The reference program is written for one: setup_inputs(seed, part) draws one part's arguments, and reference() takes and returns one part's arrays. A program takes and returns all parts, laid end to end along the dimension named above; each array names one. Nothing has to cross between parts.
Inputs may be any that keep to these rules, and one draw needn't show every extreme that they name: For each level, all leaves in the same child of a node hold the same rows of that node's coupling inverse (the first child the upper 128 rows, the second the lower).
All inputs are finite; a program needn't handle non-finite values.
Results may differ from the reference program's by a relative error of at most 0.013.
Values may be sent and summed in bfloat16 or wider, within the bound.
No kernel may reach another device: no remote copies, remote signals or barrier semaphores. Data moves between devices by JAX's collectives and lax.ppermute only.
A program may use at most 64 MiB of HBM per device.

```python
import jax
import jax.numpy as jnp

LEAF = 512
RANK = 128
TEMPLATES = 1024
LEAVES = 16
PIXELS = 8192
LEVELS = 4


def draw_coupling(key, part):
    leaf_ids = jnp.arange(LEAVES)
    blocks = []
    for section in range(LEVELS):
        nodes = LEAVES // 2 ** (section + 1)
        subkey = jax.random.fold_in(key, 17 + section)
        base = jax.random.normal(subkey, (nodes, 2, RANK, 2 * RANK), jnp.float32)
        base = jnp.clip(base * (2.0 * RANK) ** (-0.5), -1.0, 1.0)
        node_ids = leaf_ids // 2 ** (section + 1)
        side_ids = leaf_ids // 2 ** section % 2
        blocks.append(base[node_ids, side_ids])
    return jnp.stack(blocks).astype(jnp.bfloat16)


def levels(key, shape, pieces, least, high):
    def one(position, parts):
        steps = jax.random.uniform(jax.random.fold_in(jax.random.fold_in(key, 6), position), (parts,), jnp.float32, least / len(pieces), high / len(pieces))
        return jnp.repeat(jnp.exp(steps), shape[position] // parts).reshape((-1,) + (1,) * (len(shape) - position - 1))

    loudness = one(*pieces[0])
    for cut in pieces[1:]:
        loudness = loudness * one(*cut)
    return loudness


def noise(stream_key, dims, deviation, reach, shards=(), kind=jnp.bfloat16):
    entries = deviation * jax.random.normal(stream_key, dims, jnp.float32)
    if shards:
        entries = entries * levels(stream_key, dims, shards, -0.22, 0.18)
    return jnp.clip(entries, -reach, reach).astype(kind)


def setup_inputs(seed: int = 0, part: int = 0) -> dict:
    seeds = jax.random.split(jax.random.key(seed), 6)
    part_keys = jax.random.split(jax.random.fold_in(seeds[5], part), 6)
    templates = noise(part_keys[0], (PIXELS, TEMPLATES), 1.0, 6.0, ((0, 16),))
    leaf_inverse = noise(part_keys[1], (PIXELS, LEAF), LEAF ** -0.5, 0.25, ((0, 16),))
    v_basis = noise(part_keys[2], (LEVELS, PIXELS, RANK), (PIXELS // 2) ** -0.5, 0.09375, ((1, 16),))
    u_basis = noise(part_keys[3], (LEVELS, PIXELS, RANK), RANK ** -0.5, 0.5, ((1, 16),))
    coupling = draw_coupling(jax.random.fold_in(jax.random.fold_in(seeds[5], part), 71), part)
    return {"templates": templates, "leaf_inverse": leaf_inverse, "v_basis": v_basis, "u_basis": u_basis, "coupling": coupling}


def reference(templates, leaf_inverse, v_basis, u_basis, coupling):
    leaves = PIXELS // LEAF
    inverse_blocks = leaf_inverse.reshape(leaves, LEAF, LEAF).astype(jnp.float32)
    source = templates.reshape(leaves, LEAF, TEMPLATES).astype(jnp.float32)
    current = jnp.einsum("nij,njt->nit", inverse_blocks, source)
    for section in range(LEVELS):
        group = 2 ** section
        nodes = leaves // (2 * group)
        rounded = current.astype(jnp.bfloat16).astype(jnp.float32)
        v_blocks = v_basis[section].reshape(leaves, LEAF, RANK).astype(jnp.float32)
        partial_terms = jnp.einsum("nir,nit->nrt", v_blocks, rounded)
        projection = partial_terms.reshape(nodes, 2, group, RANK, TEMPLATES).sum(axis=2)
        stacked = projection.astype(jnp.bfloat16).reshape(nodes, 2 * RANK, TEMPLATES)
        spread = jnp.repeat(stacked, 2 * group, axis=0).astype(jnp.float32)
        coefficients = jnp.einsum("nrk,nkt->nrt", coupling[section].astype(jnp.float32), spread)
        coefficients = coefficients.astype(jnp.bfloat16).astype(jnp.float32)
        u_blocks = u_basis[section].reshape(leaves, LEAF, RANK).astype(jnp.float32)
        current = current - jnp.einsum("nir,nrt->nit", u_blocks, coefficients)
    return current.reshape(PIXELS, TEMPLATES).astype(jnp.bfloat16)
```

```python
import jax
import jax.numpy as jnp
from jax import lax
from jax.sharding import PartitionSpec as P

F32 = jnp.float32
BF16 = jnp.bfloat16


def bit_axes():
    bits = []
    for axis in ("inner", "narrow", "wide"):
        for stride in range(lax.axis_size(axis).bit_length() - 1):
            bits.append((axis, stride))
    return bits


def swap(x, bit, bits):
    axis, stride = bits[bit]
    n = lax.axis_size(axis)
    return lax.ppermute(x, axis, [(i, i ^ (1 << stride)) for i in range(n)])


def side(bit, bits):
    axis, stride = bits[bit]
    return (lax.axis_index(axis) >> stride) & 1


def cols(x, start, width):
    return lax.dynamic_slice_in_dim(x, start, width, axis=x.ndim - 1)


def reduce_half(x, bit, bits):
    w = x.shape[-1] // 2
    h = side(bit, bits)
    keep = cols(x, h * w, w)
    send = cols(x, (1 - h) * w, w)
    return keep + swap(send, bit, bits)


def gather_half(x, bit, bits):
    w = x.shape[-1]
    h = side(bit, bits)
    both = jnp.concatenate([x, swap(x, bit, bits), x], axis=-1)
    return cols(both, h * w, 2 * w)


def hi_lo(w):
    hi = w.astype(BF16)
    lo = (w - hi.astype(F32)).astype(BF16)
    return hi, lo


def on_device(templates, leaf_inverse, v_basis, u_basis, coupling):
    bits = bit_axes()
    levels, pixels, rank = v_basis.shape
    c0 = jnp.dot(leaf_inverse, templates, preferred_element_type=F32)
    c0b = c0.astype(BF16)
    proj = jnp.einsum("lir,it->lrt", v_basis, c0b, preferred_element_type=F32)
    cross = jnp.einsum("lir,kis->lkrs", v_basis, u_basis, preferred_element_type=F32)

    couple = []
    for s in range(levels):
        lower = side(s, bits) == 0
        mine = coupling[s, 0]
        theirs = swap(mine, s, bits)
        rows = []
        for c in (mine, theirs):
            rolled = jnp.concatenate([c[:, rank:], c[:, :rank]], axis=1)
            rows.append(jnp.where(lower, c, rolled))
        couple.append(jnp.concatenate(rows, axis=0))

    weights = []
    for s in range(levels - 1):
        w = cross[s + 1:, s].reshape((levels - 1 - s) * rank, rank)
        for j in range(s):
            w = w + swap(w, j, bits)
        w_sib = swap(w, s, bits)
        parts = hi_lo(w) + hi_lo(w_sib)
        weights.append(jnp.concatenate(parts, axis=1))

    rest = proj[1:]
    if levels > 1:
        rest = reduce_half(rest, 0, bits)
    own_coefs = []
    for s in range(levels):
        if s == 0:
            mine = proj[0]
        else:
            mine = rest[0]
            rest = rest[1:]
            if rest.shape[0] > 0:
                rest = reduce_half(rest, s, bits)
        mine_b = mine.astype(BF16)
        stacked = jnp.concatenate([mine_b, swap(mine_b, s, bits)], axis=0)
        coefs = jnp.dot(couple[s], stacked, preferred_element_type=F32).astype(BF16)
        own_coefs.append(coefs[:rank])
        if s < levels - 1:
            w = coefs.shape[1] // 2
            half = cols(coefs, side(s, bits) * w, w)
            co, cs = half[:rank], half[rank:]
            fix = jnp.dot(
                weights[s],
                jnp.concatenate([co, co, cs, cs], axis=0),
                preferred_element_type=F32,
            )
            rest = rest - fix.reshape(rest.shape)

    full = []
    for s in range(levels):
        c = own_coefs[s]
        for j in reversed(range(s)):
            c = gather_half(c, j, bits)
        full.append(c)
    u_all = jnp.transpose(u_basis, (1, 0, 2)).reshape(pixels, levels * rank)
    early = levels - 1
    current = c0
    if early > 0:
        current = current - jnp.dot(
            u_all[:, : early * rank],
            jnp.concatenate(full[:early], axis=0),
            preferred_element_type=F32,
        )
    current = current - jnp.dot(
        u_basis[levels - 1], full[levels - 1], preferred_element_type=F32
    )
    return current.astype(BF16)


def solution(mesh):
    placed = (
        P(("slab", "wide", "narrow", "inner"), None),
        P(("slab", "wide", "narrow", "inner"), None),
        P(None, ("slab", "wide", "narrow", "inner"), None),
        P(None, ("slab", "wide", "narrow", "inner"), None),
        P(None, ("slab", "wide", "narrow", "inner"), None, None),
    )
    return jax.shard_map(
        on_device,
        mesh=mesh,
        in_specs=placed,
        out_specs=P(("slab", "wide", "narrow", "inner"), None),
        check_vma=False,
    )
```

```python
import jax
import jax.numpy as jnp
from jax import lax
from jax.sharding import PartitionSpec as P

F32 = jnp.float32
BF16 = jnp.bfloat16


def bit_axes():
    bits = []
    for axis in ("inner", "narrow", "wide"):
        for stride in range(lax.axis_size(axis).bit_length() - 1):
            bits.append((axis, stride))
    return bits


def swap(x, bit, bits):
    axis, stride = bits[bit]
    n = lax.axis_size(axis)
    return lax.ppermute(x, axis, [(i, i ^ (1 << stride)) for i in range(n)])


def side(bit, bits):
    axis, stride = bits[bit]
    return (lax.axis_index(axis) >> stride) & 1


def cols(x, start, width):
    return lax.dynamic_slice_in_dim(x, start, width, axis=x.ndim - 1)


def reduce_half(x, bit, bits):
    w = x.shape[-1] // 2
    h = side(bit, bits)
    keep = cols(x, h * w, w)
    send = cols(x, (1 - h) * w, w)
    return keep + swap(send, bit, bits)


def gather_half(x, bit, bits):
    w = x.shape[-1]
    h = side(bit, bits)
    both = jnp.concatenate([x, swap(x, bit, bits), x], axis=-1)
    return cols(both, h * w, 2 * w)


def on_device(templates, leaf_inverse, v_basis, u_basis, coupling):
    bits = bit_axes()
    levels, pixels, rank = v_basis.shape
    width = templates.shape[1]
    c0 = jnp.dot(leaf_inverse, templates, preferred_element_type=F32)
    c0b = c0.astype(BF16)

    cross = jnp.einsum("lir,kis->lkrs", v_basis, u_basis, preferred_element_type=F32)
    mine_c = coupling[:, 0]
    partial = [cross[s + 1:, s].reshape(-1, rank) for s in range(levels - 1)]
    w_own, theirs_c = [None] * levels, []
    for b in range(levels):
        c = mine_c[b]
        parts = [jnp.concatenate([c[:, :rank], c[:, rank:]], axis=0).astype(F32)]
        parts += partial[b:]
        got = swap(jnp.concatenate(parts, axis=0), b, bits)
        theirs = got[: 2 * rank].astype(BF16)
        theirs_c.append(jnp.concatenate([theirs[:rank], theirs[rank:]], axis=1))
        at = 2 * rank
        for s in range(b, levels - 1):
            n = partial[s].shape[0]
            recv = got[at : at + n]
            at += n
            if s == b:
                w_own[s] = jnp.concatenate([partial[s], recv], axis=1)
            else:
                partial[s] = partial[s] + recv
    theirs_c = jnp.stack(theirs_c)
    lower = jnp.stack([side(s, bits) == 0 for s in range(levels)])[:, None, None]
    first = jnp.concatenate([mine_c[:, :, :rank], theirs_c[:, :, :rank]], axis=1)
    second = jnp.concatenate([mine_c[:, :, rank:], theirs_c[:, :, rank:]], axis=1)
    couple = jnp.concatenate(
        [jnp.where(lower, first, second), jnp.where(lower, second, first)], axis=2
    )

    proj0 = jnp.dot(v_basis[0].T, c0b, preferred_element_type=F32)
    rest = None
    if levels > 1:
        half = width // 2
        h = side(0, bits)
        keep = jnp.einsum(
            "lir,it->lrt", v_basis[1:], cols(c0b, h * half, half),
            preferred_element_type=F32,
        )
        send = jnp.einsum(
            "lir,it->lrt", v_basis[1:], cols(c0b, (1 - h) * half, half),
            preferred_element_type=F32,
        )
        rest = keep + swap(send, 0, bits)
    own_coefs = []
    for s in range(levels):
        if s == 0:
            mine = proj0
        else:
            mine = rest[0]
            rest = rest[1:]
            if rest.shape[0] > 0:
                rest = reduce_half(rest, s, bits)
        mine_b = mine.astype(BF16)
        stacked = jnp.concatenate([mine_b, swap(mine_b, s, bits)], axis=0)
        coefs = jnp.dot(couple[s], stacked, preferred_element_type=F32).astype(BF16)
        own_coefs.append(coefs[:rank])
        if s < levels - 1:
            w = coefs.shape[1] // 2
            piece = cols(coefs, side(s, bits) * w, w).astype(F32)
            fix = jnp.dot(
                w_own[s], piece, preferred_element_type=F32,
                precision=lax.Precision.HIGHEST,
            )
            rest = rest - fix.reshape(rest.shape)

    full = [own_coefs[0]] + [None] * (levels - 1)
    pending = {s: own_coefs[s] for s in range(1, levels)}
    for j in reversed(range(levels - 1)):
        group = [s for s in range(j + 1, levels)]
        joined = gather_half(jnp.stack([pending[s] for s in group]), j, bits)
        for i, s in enumerate(group):
            pending[s] = joined[i]
    for s in range(1, levels):
        full[s] = pending[s]
    current = c0
    for s in range(levels):
        current = current - jnp.dot(u_basis[s], full[s], preferred_element_type=F32)
    return current.astype(BF16)


def solution(mesh):
    placed = (
        P(("slab", "wide", "narrow", "inner"), None),
        P(("slab", "wide", "narrow", "inner"), None),
        P(None, ("slab", "wide", "narrow", "inner"), None),
        P(None, ("slab", "wide", "narrow", "inner"), None),
        P(None, ("slab", "wide", "narrow", "inner"), None, None),
    )
    return jax.shard_map(
        on_device,
        mesh=mesh,
        in_specs=placed,
        out_specs=P(("slab", "wide", "narrow", "inner"), None),
        check_vma=False,
    )
```

```python
import jax
import jax.numpy as jnp
from jax import lax
from jax.sharding import PartitionSpec as P

F32 = jnp.float32
BF16 = jnp.bfloat16


def bit_axes():
    bits = []
    for axis in ("inner", "narrow", "wide"):
        for stride in range(lax.axis_size(axis).bit_length() - 1):
            bits.append((axis, stride))
    return bits


def swap(x, bit, bits):
    axis, stride = bits[bit]
    n = lax.axis_size(axis)
    return lax.ppermute(x, axis, [(i, i ^ (1 << stride)) for i in range(n)])


def side(bit, bits):
    axis, stride = bits[bit]
    return (lax.axis_index(axis) >> stride) & 1


def cols(x, start, width):
    return lax.dynamic_slice_in_dim(x, start, width, axis=x.ndim - 1)


def reduce_half(x, bit, bits):
    w = x.shape[-1] // 2
    h = side(bit, bits)
    keep = cols(x, h * w, w)
    send = cols(x, (1 - h) * w, w)
    return keep + swap(send, bit, bits)


def gather_half(x, bit, bits):
    w = x.shape[-1]
    h = side(bit, bits)
    both = jnp.concatenate([x, swap(x, bit, bits), x], axis=-1)
    return cols(both, h * w, 2 * w)


def on_device(templates, leaf_inverse, v_basis, u_basis, coupling):
    bits = bit_axes()
    levels, pixels, rank = v_basis.shape
    width = templates.shape[1]
    c0 = jnp.dot(leaf_inverse, templates, preferred_element_type=F32)
    c0b = c0.astype(BF16)

    mine_c = coupling[:, 0]
    partial = [
        jnp.einsum(
            "lir,is->lrs", v_basis[s + 1:], u_basis[s], preferred_element_type=F32
        ).reshape(-1, rank)
        for s in range(levels - 1)
    ]
    w_own, theirs_c = [None] * levels, []
    for b in range(levels):
        c = mine_c[b]
        parts = [jnp.concatenate([c[:, :rank], c[:, rank:]], axis=0).astype(F32)]
        parts += partial[b:]
        got = swap(jnp.concatenate(parts, axis=0), b, bits)
        theirs = got[: 2 * rank].astype(BF16)
        theirs_c.append(jnp.concatenate([theirs[:rank], theirs[rank:]], axis=1))
        at = 2 * rank
        for s in range(b, levels - 1):
            n = partial[s].shape[0]
            recv = got[at : at + n]
            at += n
            if s == b:
                w_own[s] = jnp.concatenate([partial[s], recv], axis=1)
            else:
                partial[s] = partial[s] + recv
    couple = []
    for s in range(levels):
        lower = side(s, bits) == 0
        mine, theirs = mine_c[s], theirs_c[s]
        first = jnp.concatenate([mine[:, :rank], theirs[:, :rank]], axis=0)
        second = jnp.concatenate([mine[:, rank:], theirs[:, rank:]], axis=0)
        couple.append(
            jnp.concatenate(
                [jnp.where(lower, first, second), jnp.where(lower, second, first)],
                axis=1,
            )
        )

    proj0 = jnp.dot(v_basis[0].T, c0b, preferred_element_type=F32)
    rest = None
    if levels > 1:
        half = width // 2
        h = side(0, bits)
        keep = jnp.einsum(
            "lir,it->lrt", v_basis[1:], cols(c0b, h * half, half),
            preferred_element_type=F32,
        )
        send = jnp.einsum(
            "lir,it->lrt", v_basis[1:], cols(c0b, (1 - h) * half, half),
            preferred_element_type=F32,
        )
        rest = keep + swap(send, 0, bits)
    own_coefs = []
    for s in range(levels):
        if s == 0:
            mine = proj0
        else:
            mine = rest[0]
            rest = rest[1:]
            if rest.shape[0] > 0:
                rest = reduce_half(rest, s, bits)
        mine_b = mine.astype(BF16)
        stacked = jnp.concatenate([mine_b, swap(mine_b, s, bits)], axis=0)
        coefs = jnp.dot(couple[s], stacked, preferred_element_type=F32).astype(BF16)
        own_coefs.append(coefs[:rank])
        if s < levels - 1:
            w = coefs.shape[1] // 2
            piece = cols(coefs, side(s, bits) * w, w).astype(F32)
            fix = jnp.dot(
                w_own[s], piece, preferred_element_type=F32,
                precision=lax.Precision.HIGHEST,
            )
            rest = rest - fix.reshape(rest.shape)

    full = [own_coefs[0]] + [None] * (levels - 1)
    pending = {s: own_coefs[s] for s in range(1, levels)}
    for j in reversed(range(levels - 1)):
        group = [s for s in range(j + 1, levels)]
        joined = gather_half(jnp.stack([pending[s] for s in group]), j, bits)
        for i, s in enumerate(group):
            pending[s] = joined[i]
    for s in range(1, levels):
        full[s] = pending[s]
    current = c0
    for s in range(levels):
        current = current - jnp.dot(u_basis[s], full[s], preferred_element_type=F32)
    return current.astype(BF16)


def solution(mesh):
    placed = (
        P(("slab", "wide", "narrow", "inner"), None),
        P(("slab", "wide", "narrow", "inner"), None),
        P(None, ("slab", "wide", "narrow", "inner"), None),
        P(None, ("slab", "wide", "narrow", "inner"), None),
        P(None, ("slab", "wide", "narrow", "inner"), None, None),
    )
    return jax.shard_map(
        on_device,
        mesh=mesh,
        in_specs=placed,
        out_specs=P(("slab", "wide", "narrow", "inner"), None),
        check_vma=False,
    )
```

```python
import jax
import jax.numpy as jnp
from jax import lax
from jax.sharding import PartitionSpec as P

F32 = jnp.float32
BF16 = jnp.bfloat16


def bit_axes():
    bits = []
    for axis in ("inner", "narrow", "wide"):
        for stride in range(lax.axis_size(axis).bit_length() - 1):
            bits.append((axis, stride))
    return bits


def swap(x, bit, bits):
    axis, stride = bits[bit]
    n = lax.axis_size(axis)
    return lax.ppermute(x, axis, [(i, i ^ (1 << stride)) for i in range(n)])


def side(bit, bits):
    axis, stride = bits[bit]
    return (lax.axis_index(axis) >> stride) & 1


def cols(x, start, width):
    return lax.dynamic_slice_in_dim(x, start, width, axis=x.ndim - 1)


def reduce_half(x, bit, bits):
    w = x.shape[-1] // 2
    h = side(bit, bits)
    keep = cols(x, h * w, w)
    send = cols(x, (1 - h) * w, w)
    return keep + swap(send, bit, bits)


def gather_half(x, bit, bits):
    w = x.shape[-1]
    h = side(bit, bits)
    both = jnp.concatenate([x, swap(x, bit, bits), x], axis=-1)
    return cols(both, h * w, 2 * w)


def on_device(templates, leaf_inverse, v_basis, u_basis, coupling):
    bits = bit_axes()
    levels, pixels, rank = v_basis.shape
    width = templates.shape[1]
    c0 = jnp.dot(leaf_inverse, templates, preferred_element_type=F32)
    c0b = c0.astype(BF16)

    mine_c = coupling[:, 0]
    partial = [
        jnp.einsum(
            "lir,is->lrs", v_basis[s + 1:], u_basis[s], preferred_element_type=F32
        ).reshape(-1, rank)
        for s in range(levels - 1)
    ]
    w_own, theirs_c = [None] * levels, []
    for b in range(levels):
        c = mine_c[b]
        parts = [jnp.concatenate([c[:, :rank], c[:, rank:]], axis=0).astype(F32)]
        parts += partial[b:]
        got = swap(jnp.concatenate(parts, axis=0), b, bits)
        theirs = got[: 2 * rank].astype(BF16)
        theirs_c.append(jnp.concatenate([theirs[:rank], theirs[rank:]], axis=1))
        at = 2 * rank
        for s in range(b, levels - 1):
            n = partial[s].shape[0]
            recv = got[at : at + n]
            at += n
            if s == b:
                w_own[s] = jnp.concatenate([partial[s], recv], axis=1)
            else:
                partial[s] = partial[s] + recv
    couple = []
    for s in range(levels):
        lower = side(s, bits) == 0
        mine, theirs = mine_c[s], theirs_c[s]
        first = jnp.concatenate([mine[:, :rank], theirs[:, :rank]], axis=0)
        second = jnp.concatenate([mine[:, rank:], theirs[:, rank:]], axis=0)
        couple.append(
            jnp.concatenate(
                [jnp.where(lower, first, second), jnp.where(lower, second, first)],
                axis=1,
            )
        )

    proj0 = jnp.dot(v_basis[0].T, c0b, preferred_element_type=F32)
    rest = None
    if levels > 1:
        half = width // 2
        h = side(0, bits)
        keep = jnp.einsum(
            "lir,it->lrt", v_basis[1:], cols(c0b, h * half, half),
            preferred_element_type=F32,
        )
        send = jnp.einsum(
            "lir,it->lrt", v_basis[1:], cols(c0b, (1 - h) * half, half),
            preferred_element_type=F32,
        )
        rest = keep + swap(send, 0, bits)
    own_coefs = []
    for s in range(levels):
        if s == 0:
            mine_b = proj0.astype(BF16)
            theirs_b = swap(mine_b, s, bits)
        else:
            mine_b = rest[0].astype(BF16)
            rest = rest[1:]
            n = rest.shape[0]
            w = mine_b.shape[1] // 2
            parts = [mine_b[:, :w], mine_b[:, w:]]
            if n > 0:
                h = side(s, bits)
                keep = cols(rest, h * w, w)
                send = cols(rest, (1 - h) * w, w)
                parts.append(send.astype(BF16).reshape(n * rank, w))
            got = swap(jnp.concatenate(parts, axis=0), s, bits)
            theirs_b = jnp.concatenate([got[:rank], got[rank : 2 * rank]], axis=1)
            if n > 0:
                recv = got[2 * rank :].reshape(n, rank, w).astype(F32)
                rest = keep + recv
        stacked = jnp.concatenate([mine_b, theirs_b], axis=0)
        coefs = jnp.dot(couple[s], stacked, preferred_element_type=F32).astype(BF16)
        own_coefs.append(coefs[:rank])
        if s < levels - 1:
            w = coefs.shape[1] // 2
            piece = cols(coefs, side(s, bits) * w, w).astype(F32)
            fix = jnp.dot(
                w_own[s], piece, preferred_element_type=F32,
                precision=lax.Precision.HIGHEST,
            )
            rest = rest - fix.reshape(rest.shape)

    full = [own_coefs[0]] + [None] * (levels - 1)
    pending = {s: own_coefs[s] for s in range(1, levels)}
    for j in reversed(range(levels - 1)):
        group = [s for s in range(j + 1, levels)]
        joined = gather_half(jnp.stack([pending[s] for s in group]), j, bits)
        for i, s in enumerate(group):
            pending[s] = joined[i]
    for s in range(1, levels):
        full[s] = pending[s]
    current = c0
    for s in range(levels):
        current = current - jnp.dot(u_basis[s], full[s], preferred_element_type=F32)
    return current.astype(BF16)


def solution(mesh):
    placed = (
        P(("slab", "wide", "narrow", "inner"), None),
        P(("slab", "wide", "narrow", "inner"), None),
        P(None, ("slab", "wide", "narrow", "inner"), None),
        P(None, ("slab", "wide", "narrow", "inner"), None),
        P(None, ("slab", "wide", "narrow", "inner"), None, None),
    )
    return jax.shard_map(
        on_device,
        mesh=mesh,
        in_specs=placed,
        out_specs=P(("slab", "wide", "narrow", "inner"), None),
        check_vma=False,
    )
```

```python
import jax
import jax.numpy as jnp
from jax import lax
from jax.sharding import PartitionSpec as P

F32 = jnp.float32
BF16 = jnp.bfloat16


def bit_axes():
    bits = []
    for axis in ("inner", "narrow", "wide"):
        for stride in range(lax.axis_size(axis).bit_length() - 1):
            bits.append((axis, stride))
    return bits


def swap(x, bit, bits):
    axis, stride = bits[bit]
    n = lax.axis_size(axis)
    return lax.ppermute(x, axis, [(i, i ^ (1 << stride)) for i in range(n)])


def side(bit, bits):
    axis, stride = bits[bit]
    return (lax.axis_index(axis) >> stride) & 1


def cols(x, start, width):
    return lax.dynamic_slice_in_dim(x, start, width, axis=x.ndim - 1)


def reduce_half(x, bit, bits):
    w = x.shape[-1] // 2
    h = side(bit, bits)
    keep = cols(x, h * w, w)
    send = cols(x, (1 - h) * w, w)
    return keep + swap(send, bit, bits)


def gather_half(x, bit, bits):
    w = x.shape[-1]
    h = side(bit, bits)
    both = jnp.concatenate([x, swap(x, bit, bits), x], axis=-1)
    return cols(both, h * w, 2 * w)


def on_device(templates, leaf_inverse, v_basis, u_basis, coupling):
    bits = bit_axes()
    levels, pixels, rank = v_basis.shape
    width = templates.shape[1]
    c0 = jnp.dot(leaf_inverse, templates, preferred_element_type=F32)
    c0b = c0.astype(BF16)

    partial = [
        jnp.einsum(
            "lir,is->lrs", v_basis[s + 1:], u_basis[s], preferred_element_type=F32
        ).reshape(-1, rank)
        for s in range(levels - 1)
    ]
    w_own = [None] * levels
    for b in range(levels - 1):
        got = swap(jnp.concatenate(partial[b:], axis=0), b, bits)
        at = 0
        for s in range(b, levels - 1):
            n = partial[s].shape[0]
            recv = got[at : at + n]
            at += n
            if s == b:
                w_own[s] = jnp.concatenate([partial[s], recv], axis=1)
            else:
                partial[s] = partial[s] + recv

    couple_own, couple_send = [], []
    for s in range(levels):
        lower = side(s, bits) == 0
        c = coupling[s, 0]
        rolled = jnp.concatenate([c[:, rank:], c[:, :rank]], axis=1)
        couple_own.append(jnp.where(lower, c, rolled))
        couple_send.append(jnp.where(lower, rolled, c))

    proj0 = jnp.dot(v_basis[0].T, c0b, preferred_element_type=F32)
    rest = None
    if levels > 1:
        half = width // 2
        h = side(0, bits)
        keep = jnp.einsum(
            "lir,it->lrt", v_basis[1:], cols(c0b, h * half, half),
            preferred_element_type=F32,
        )
        send = jnp.einsum(
            "lir,it->lrt", v_basis[1:], cols(c0b, (1 - h) * half, half),
            preferred_element_type=F32,
        )
        rest = keep + swap(send, 0, bits)
    own_coefs = []
    for s in range(levels):
        if s == 0:
            mine_b = proj0.astype(BF16)
            theirs_b = swap(mine_b, s, bits)
            couple_sib = swap(couple_send[0], s, bits)
        else:
            mine_b = rest[0].astype(BF16)
            rest = rest[1:]
            n = rest.shape[0]
            w = mine_b.shape[1] // 2
            parts = [mine_b[:, :w], mine_b[:, w:]]
            if n > 0:
                h = side(s, bits)
                keep = cols(rest, h * w, w)
                send = cols(rest, (1 - h) * w, w)
                parts.append(send.astype(BF16).reshape(n * rank, w))
            parts.append(couple_send[s].reshape(-1, w))
            got = swap(jnp.concatenate(parts, axis=0), s, bits)
            theirs_b = jnp.concatenate([got[:rank], got[rank : 2 * rank]], axis=1)
            at = 2 * rank
            if n > 0:
                recv = got[at : at + n * rank].reshape(n, rank, w).astype(F32)
                rest = keep + recv
                at += n * rank
            couple_sib = got[at:].reshape(rank, 2 * rank)
        stacked = jnp.concatenate([mine_b, theirs_b], axis=0)
        couple = jnp.concatenate([couple_own[s], couple_sib], axis=0)
        coefs = jnp.dot(couple, stacked, preferred_element_type=F32).astype(BF16)
        own_coefs.append(coefs[:rank])
        if s < levels - 1:
            w = coefs.shape[1] // 2
            piece = cols(coefs, side(s, bits) * w, w).astype(F32)
            fix = jnp.dot(
                w_own[s], piece, preferred_element_type=F32,
                precision=lax.Precision.HIGHEST,
            )
            rest = rest - fix.reshape(rest.shape)

    full = [own_coefs[0]] + [None] * (levels - 1)
    pending = {s: own_coefs[s] for s in range(1, levels)}
    for j in reversed(range(levels - 1)):
        group = [s for s in range(j + 1, levels)]
        joined = gather_half(jnp.stack([pending[s] for s in group]), j, bits)
        for i, s in enumerate(group):
            pending[s] = joined[i]
    for s in range(1, levels):
        full[s] = pending[s]
    current = c0
    for s in range(levels):
        current = current - jnp.dot(u_basis[s], full[s], preferred_element_type=F32)
    return current.astype(BF16)


def solution(mesh):
    placed = (
        P(("slab", "wide", "narrow", "inner"), None),
        P(("slab", "wide", "narrow", "inner"), None),
        P(None, ("slab", "wide", "narrow", "inner"), None),
        P(None, ("slab", "wide", "narrow", "inner"), None),
        P(None, ("slab", "wide", "narrow", "inner"), None, None),
    )
    return jax.shard_map(
        on_device,
        mesh=mesh,
        in_specs=placed,
        out_specs=P(("slab", "wide", "narrow", "inner"), None),
        check_vma=False,
    )
```

```python
import jax
import jax.numpy as jnp
from jax import lax
from jax.sharding import PartitionSpec as P

F32 = jnp.float32
BF16 = jnp.bfloat16


def bit_axes():
    bits = []
    for axis in ("inner", "narrow", "wide"):
        for stride in range(lax.axis_size(axis).bit_length() - 1):
            bits.append((axis, stride))
    return bits


def swap(x, bit, bits):
    axis, stride = bits[bit]
    n = lax.axis_size(axis)
    return lax.ppermute(x, axis, [(i, i ^ (1 << stride)) for i in range(n)])


def side(bit, bits):
    axis, stride = bits[bit]
    return (lax.axis_index(axis) >> stride) & 1


def cols(x, start, width):
    return lax.dynamic_slice_in_dim(x, start, width, axis=x.ndim - 1)


def reduce_half(x, bit, bits):
    w = x.shape[-1] // 2
    h = side(bit, bits)
    keep = cols(x, h * w, w)
    send = cols(x, (1 - h) * w, w)
    return keep + swap(send, bit, bits)


def gather_half(x, bit, bits):
    w = x.shape[-1]
    h = side(bit, bits)
    both = jnp.concatenate([x, swap(x, bit, bits), x], axis=-1)
    return cols(both, h * w, 2 * w)


def on_device(templates, leaf_inverse, v_basis, u_basis, coupling):
    bits = bit_axes()
    levels, pixels, rank = v_basis.shape
    width = templates.shape[1]
    c0 = jnp.dot(leaf_inverse, templates, preferred_element_type=F32)
    c0b = c0.astype(BF16)

    partial = [
        jnp.einsum(
            "lir,is->lrs", v_basis[s + 1:], u_basis[s], preferred_element_type=F32
        ).reshape(-1, rank)
        for s in range(levels - 1)
    ]
    w_own = [None] * levels
    for b in range(levels - 1):
        got = swap(jnp.concatenate(partial[b:], axis=0), b, bits)
        at = 0
        for s in range(b, levels - 1):
            n = partial[s].shape[0]
            recv = got[at : at + n]
            at += n
            if s == b:
                w_own[s] = jnp.concatenate([partial[s], recv], axis=1)
            else:
                partial[s] = partial[s] + recv

    couple_own, couple_send = [], []
    for s in range(levels):
        lower = side(s, bits) == 0
        c = coupling[s, 0]
        rolled = jnp.concatenate([c[:, rank:], c[:, :rank]], axis=1)
        couple_own.append(jnp.where(lower, c, rolled))
        couple_send.append(jnp.where(lower, rolled, c))

    proj0 = jnp.dot(v_basis[0].T, c0b, preferred_element_type=F32)
    rest = None
    if levels > 1:
        half = width // 2
        h = side(0, bits)
        keep = jnp.einsum(
            "lir,it->lrt", v_basis[1:], cols(c0b, h * half, half),
            preferred_element_type=F32,
        )
        send = jnp.einsum(
            "lir,it->lrt", v_basis[1:], cols(c0b, (1 - h) * half, half),
            preferred_element_type=F32,
        )
        rest = keep + swap(send, 0, bits)
    own_coefs = []
    for s in range(levels):
        if s == 0:
            mine_b = proj0.astype(BF16)
            theirs_b = swap(mine_b, s, bits)
            couple_sib = swap(couple_send[0], s, bits)
        else:
            mine_b = rest[0].astype(BF16)
            rest = rest[1:]
            n = rest.shape[0]
            w = mine_b.shape[1] // 2
            parts = [mine_b[:, :w], mine_b[:, w:]]
            if n > 0:
                h = side(s, bits)
                keep = cols(rest, h * w, w)
                send = cols(rest, (1 - h) * w, w)
                parts.append(send.astype(BF16).reshape(n * rank, w))
            parts.append(couple_send[s].reshape(-1, w))
            payload = jnp.concatenate(parts, axis=0)
            if s < levels - 1:
                payload, w_own[s] = lax.optimization_barrier((payload, w_own[s]))
            got = swap(payload, s, bits)
            theirs_b = jnp.concatenate([got[:rank], got[rank : 2 * rank]], axis=1)
            at = 2 * rank
            if n > 0:
                recv = got[at : at + n * rank].reshape(n, rank, w).astype(F32)
                rest = keep + recv
                at += n * rank
            couple_sib = got[at:].reshape(rank, 2 * rank)
        stacked = jnp.concatenate([mine_b, theirs_b], axis=0)
        couple = jnp.concatenate([couple_own[s], couple_sib], axis=0)
        coefs = jnp.dot(couple, stacked, preferred_element_type=F32).astype(BF16)
        own_coefs.append(coefs[:rank])
        if s < levels - 1:
            w = coefs.shape[1] // 2
            piece = cols(coefs, side(s, bits) * w, w).astype(F32)
            fix = jnp.dot(
                w_own[s], piece, preferred_element_type=F32,
                precision=lax.Precision.HIGHEST,
            )
            rest = rest - fix.reshape(rest.shape)

    full = [own_coefs[0]] + [None] * (levels - 1)
    pending = {s: own_coefs[s] for s in range(1, levels)}
    for j in reversed(range(levels - 1)):
        group = [s for s in range(j + 1, levels)]
        joined = gather_half(jnp.stack([pending[s] for s in group]), j, bits)
        for i, s in enumerate(group):
            pending[s] = joined[i]
    for s in range(1, levels):
        full[s] = pending[s]
    current = c0
    for s in range(levels):
        current = current - jnp.dot(u_basis[s], full[s], preferred_element_type=F32)
    return current.astype(BF16)


def solution(mesh):
    placed = (
        P(("slab", "wide", "narrow", "inner"), None),
        P(("slab", "wide", "narrow", "inner"), None),
        P(None, ("slab", "wide", "narrow", "inner"), None),
        P(None, ("slab", "wide", "narrow", "inner"), None),
        P(None, ("slab", "wide", "narrow", "inner"), None, None),
    )
    return jax.shard_map(
        on_device,
        mesh=mesh,
        in_specs=placed,
        out_specs=P(("slab", "wide", "narrow", "inner"), None),
        check_vma=False,
    )
```

```python
import jax
import jax.numpy as jnp
from jax import lax
from jax.sharding import PartitionSpec as P

F32 = jnp.float32
BF16 = jnp.bfloat16


def bit_axes():
    bits = []
    for axis in ("inner", "narrow", "wide"):
        for stride in range(lax.axis_size(axis).bit_length() - 1):
            bits.append((axis, stride))
    return bits


def swap(x, bit, bits):
    axis, stride = bits[bit]
    n = lax.axis_size(axis)
    return lax.ppermute(x, axis, [(i, i ^ (1 << stride)) for i in range(n)])


def side(bit, bits):
    axis, stride = bits[bit]
    return (lax.axis_index(axis) >> stride) & 1


def cols(x, start, width):
    return lax.dynamic_slice_in_dim(x, start, width, axis=x.ndim - 1)


def gather_half(x, bit, bits):
    w = x.shape[-1]
    h = side(bit, bits)
    both = jnp.concatenate([x, swap(x, bit, bits), x], axis=-1)
    return cols(both, h * w, 2 * w)


def on_device(templates, leaf_inverse, v_basis, u_basis, coupling):
    bits = bit_axes()
    levels, pixels, rank = v_basis.shape
    width = templates.shape[1]
    c0 = jnp.dot(leaf_inverse, templates, preferred_element_type=F32)
    c0b = c0.astype(BF16)

    cross = jnp.einsum("kis,lir->klrs", u_basis, v_basis, preferred_element_type=F32)
    counts = [levels - 1 - k for k in range(levels - 1)]
    suffix = jnp.concatenate(
        [cross[k, k + 1 :].reshape(-1, rank) for k in range(levels - 1)], axis=0
    )
    w_own, w_sib = [None] * levels, [None] * levels
    for b in range(levels - 1):
        n = counts[b] * rank
        got = swap(suffix, b, bits)
        w_own[b] = suffix[:n].reshape(counts[b], rank, rank)
        w_sib[b] = got[:n].reshape(counts[b], rank, rank)
        suffix = suffix[n:] + got[n:]
    couple_sib = [swap(coupling[s, 0], s, bits) for s in range(levels)]

    proj0 = jnp.dot(v_basis[0].T, c0b, preferred_element_type=F32)
    rest = None
    if levels > 1:
        half = width // 2
        h = side(0, bits)
        keep = jnp.einsum(
            "lir,it->lrt", v_basis[1:], cols(c0b, h * half, half),
            preferred_element_type=F32,
        )
        send = jnp.einsum(
            "lir,it->lrt", v_basis[1:], cols(c0b, (1 - h) * half, half),
            preferred_element_type=F32,
        )
        rest = keep + swap(send, 0, bits)
    own_coefs = []
    for s in range(levels):
        if s == 0:
            mine_b = proj0.astype(BF16)
            theirs_b = swap(mine_b, s, bits)
        else:
            mine_b = rest[0].astype(BF16)
            rest = rest[1:]
            n = rest.shape[0]
            w = mine_b.shape[1] // 2
            parts = [mine_b[:, :w], mine_b[:, w:]]
            if n > 0:
                h = side(s, bits)
                keep = cols(rest, h * w, w)
                send = cols(rest, (1 - h) * w, w)
                parts.append(send.astype(BF16).reshape(n * rank, w))
            payload = jnp.concatenate(parts, axis=0)
            if s < levels - 1:
                payload, w_sib[s] = lax.optimization_barrier((payload, w_sib[s]))
            got = swap(payload, s, bits)
            theirs_b = jnp.concatenate([got[:rank], got[rank : 2 * rank]], axis=1)
            if n > 0:
                recv = got[2 * rank :].reshape(n, rank, w).astype(F32)
                rest = keep + recv
        lower = side(s, bits) == 0
        stacked = jnp.where(
            lower,
            jnp.concatenate([mine_b, theirs_b], axis=0),
            jnp.concatenate([theirs_b, mine_b], axis=0),
        )
        couple = jnp.concatenate([coupling[s, 0], couple_sib[s]], axis=0)
        coefs = jnp.dot(couple, stacked, preferred_element_type=F32).astype(BF16)
        own_coefs.append(coefs[:rank])
        if s < levels - 1:
            w = coefs.shape[1] // 2
            piece = cols(coefs, side(s, bits) * w, w).astype(F32)
            fix = jnp.einsum(
                "nrs,st->nrt", w_own[s], piece[:rank],
                preferred_element_type=F32, precision=lax.Precision.HIGHEST,
            ) + jnp.einsum(
                "nrs,st->nrt", w_sib[s], piece[rank:],
                preferred_element_type=F32, precision=lax.Precision.HIGHEST,
            )
            rest = rest - fix

    pending = {s: own_coefs[s] for s in range(1, levels)}
    for j in reversed(range(levels - 1)):
        group = [s for s in range(j + 1, levels)]
        joined = gather_half(jnp.stack([pending[s] for s in group]), j, bits)
        for i, s in enumerate(group):
            pending[s] = joined[i]
    full = [own_coefs[0]] + [pending[s] for s in range(1, levels)]
    current = c0
    for s in range(levels):
        current = current - jnp.dot(u_basis[s], full[s], preferred_element_type=F32)
    return current.astype(BF16)


def solution(mesh):
    placed = (
        P(("slab", "wide", "narrow", "inner"), None),
        P(("slab", "wide", "narrow", "inner"), None),
        P(None, ("slab", "wide", "narrow", "inner"), None),
        P(None, ("slab", "wide", "narrow", "inner"), None),
        P(None, ("slab", "wide", "narrow", "inner"), None, None),
    )
    return jax.shard_map(
        on_device,
        mesh=mesh,
        in_specs=placed,
        out_specs=P(("slab", "wide", "narrow", "inner"), None),
        check_vma=False,
    )
```

```python
import jax
import jax.numpy as jnp
from jax import lax
from jax.sharding import PartitionSpec as P

F32 = jnp.float32
BF16 = jnp.bfloat16


def bit_axes():
    bits = []
    for axis in ("inner", "narrow", "wide"):
        for stride in range(lax.axis_size(axis).bit_length() - 1):
            bits.append((axis, stride))
    return bits


def swap(x, bit, bits):
    axis, stride = bits[bit]
    n = lax.axis_size(axis)
    return lax.ppermute(x, axis, [(i, i ^ (1 << stride)) for i in range(n)])


def side(bit, bits):
    axis, stride = bits[bit]
    return (lax.axis_index(axis) >> stride) & 1


def cols(x, start, width):
    return lax.dynamic_slice_in_dim(x, start, width, axis=x.ndim - 1)


def gather_half(x, bit, bits):
    w = x.shape[-1]
    h = side(bit, bits)
    both = jnp.concatenate([x, swap(x, bit, bits), x], axis=-1)
    return cols(both, h * w, 2 * w)


def on_device(templates, leaf_inverse, v_basis, u_basis, coupling):
    bits = bit_axes()
    levels, pixels, rank = v_basis.shape
    width = templates.shape[1]
    cross = jnp.einsum("kis,lir->klrs", u_basis, v_basis, preferred_element_type=F32)
    counts = [levels - 1 - k for k in range(levels - 1)]
    suffix = jnp.concatenate(
        [cross[k, k + 1 :].reshape(-1, rank) for k in range(levels - 1)], axis=0
    )
    w_own, m_sib = [None] * levels, [None] * levels
    for b in range(levels - 1):
        n = counts[b] * rank
        w_own[b] = suffix[:n].reshape(counts[b], rank, rank)
        m = jnp.einsum(
            "nrs,sk->nrk", w_own[b], coupling[b, 0].astype(F32),
            preferred_element_type=F32, precision=lax.Precision.HIGHEST,
        )
        later = suffix[n:]
        payload = jnp.concatenate([later, m.reshape(-1, rank)], axis=0)
        if b == 0:
            payload, templates = lax.optimization_barrier((payload, templates))
        got = swap(payload, b, bits)
        k = later.shape[0]
        m_sib[b] = got[k:].reshape(counts[b], rank, 2 * rank)
        suffix = later + got[:k]

    c0 = jnp.dot(leaf_inverse, templates, preferred_element_type=F32)
    c0b = c0.astype(BF16)
    proj0 = jnp.dot(v_basis[0].T, c0b, preferred_element_type=F32)
    rest = None
    if levels > 1:
        half = width // 2
        h = side(0, bits)
        keep = jnp.einsum(
            "lir,it->lrt", v_basis[1:], cols(c0b, h * half, half),
            preferred_element_type=F32,
        )
        send = jnp.einsum(
            "lir,it->lrt", v_basis[1:], cols(c0b, (1 - h) * half, half),
            preferred_element_type=F32,
        )
        rest = keep + swap(send, 0, bits)
    own_coefs = []
    for s in range(levels):
        if s == 0:
            mine_b = proj0.astype(BF16)
            theirs_b = swap(mine_b, s, bits)
        else:
            mine_b = rest[0].astype(BF16)
            rest = rest[1:]
            n = rest.shape[0]
            w = mine_b.shape[1] // 2
            parts = [mine_b[:, :w], mine_b[:, w:]]
            if n > 0:
                h = side(s, bits)
                keep = cols(rest, h * w, w)
                send = cols(rest, (1 - h) * w, w)
                parts.append(send.astype(BF16).reshape(n * rank, w))
            payload = jnp.concatenate(parts, axis=0)
            if s < levels - 1:
                payload, m_sib[s] = lax.optimization_barrier((payload, m_sib[s]))
            got = swap(payload, s, bits)
            theirs_b = jnp.concatenate([got[:rank], got[rank : 2 * rank]], axis=1)
            if n > 0:
                recv = got[2 * rank :].reshape(n, rank, w).astype(F32)
                rest = keep + recv
        lower = side(s, bits) == 0
        stacked = jnp.where(
            lower,
            jnp.concatenate([mine_b, theirs_b], axis=0),
            jnp.concatenate([theirs_b, mine_b], axis=0),
        )
        coefs = jnp.dot(coupling[s, 0], stacked, preferred_element_type=F32).astype(BF16)
        own_coefs.append(coefs)
        if s < levels - 1:
            w = coefs.shape[1] // 2
            h = side(s, bits)
            fix = jnp.einsum(
                "nrs,st->nrt", w_own[s], cols(coefs, h * w, w).astype(F32),
                preferred_element_type=F32, precision=lax.Precision.HIGHEST,
            ) + jnp.einsum(
                "nrk,kt->nrt", m_sib[s], cols(stacked, h * w, w).astype(F32),
                preferred_element_type=F32, precision=lax.Precision.HIGHEST,
            )
            rest = rest - fix

    pending = {s: own_coefs[s] for s in range(1, levels)}
    for j in reversed(range(levels - 1)):
        group = [s for s in range(j + 1, levels)]
        joined = gather_half(jnp.stack([pending[s] for s in group]), j, bits)
        for i, s in enumerate(group):
            pending[s] = joined[i]
    full = [own_coefs[0]] + [pending[s] for s in range(1, levels)]
    current = c0
    for s in range(levels):
        current = current - jnp.dot(u_basis[s], full[s], preferred_element_type=F32)
    return current.astype(BF16)


def solution(mesh):
    placed = (
        P(("slab", "wide", "narrow", "inner"), None),
        P(("slab", "wide", "narrow", "inner"), None),
        P(None, ("slab", "wide", "narrow", "inner"), None),
        P(None, ("slab", "wide", "narrow", "inner"), None),
        P(None, ("slab", "wide", "narrow", "inner"), None, None),
    )
    return jax.shard_map(
        on_device,
        mesh=mesh,
        in_specs=placed,
        out_specs=P(("slab", "wide", "narrow", "inner"), None),
        check_vma=False,
    )
```

```python
import jax
import jax.numpy as jnp
from jax import lax
from jax.sharding import PartitionSpec as P

F32 = jnp.float32
BF16 = jnp.bfloat16


def bit_axes():
    bits = []
    for axis in ("inner", "narrow", "wide"):
        for stride in range(lax.axis_size(axis).bit_length() - 1):
            bits.append((axis, stride))
    return bits


def swap(x, bit, bits):
    axis, stride = bits[bit]
    n = lax.axis_size(axis)
    return lax.ppermute(x, axis, [(i, i ^ (1 << stride)) for i in range(n)])


def side(bit, bits):
    axis, stride = bits[bit]
    return (lax.axis_index(axis) >> stride) & 1


def cols(x, start, width):
    return lax.dynamic_slice_in_dim(x, start, width, axis=x.ndim - 1)


def gather_half(x, bit, bits):
    w = x.shape[-1]
    h = side(bit, bits)
    both = jnp.concatenate([x, swap(x, bit, bits), x], axis=-1)
    return cols(both, h * w, 2 * w)


def on_device(templates, leaf_inverse, v_basis, u_basis, coupling):
    bits = bit_axes()
    levels, pixels, rank = v_basis.shape
    width = templates.shape[1]
    cross = jnp.einsum("kis,lir->klrs", u_basis, v_basis, preferred_element_type=F32)
    counts = [levels - 1 - k for k in range(levels - 1)]
    suffix = jnp.concatenate(
        [cross[k, k + 1 :].reshape(-1, rank) for k in range(levels - 1)], axis=0
    )
    w_own, m_sib = [None] * levels, [None] * levels
    for b in range(levels - 1):
        n = counts[b] * rank
        w_own[b] = suffix[:n].reshape(counts[b], rank, rank)
        m = jnp.einsum(
            "nrs,sk->nkr", w_own[b], coupling[b, 0].astype(F32),
            preferred_element_type=F32, precision=lax.Precision.HIGHEST,
        )
        later = suffix[n:]
        payload = jnp.concatenate([later, m.reshape(-1, rank)], axis=0)
        if b == 0:
            payload, templates = lax.optimization_barrier((payload, templates))
        got = swap(payload, b, bits)
        k = later.shape[0]
        m_sib[b] = got[k:].reshape(counts[b], 2 * rank, rank)
        suffix = later + got[:k]

    c0 = jnp.dot(leaf_inverse, templates, preferred_element_type=F32)
    c0b = c0.astype(BF16)
    proj0 = jnp.dot(v_basis[0].T, c0b, preferred_element_type=F32)
    rest = None
    if levels > 1:
        half = width // 2
        h = side(0, bits)
        keep = jnp.einsum(
            "lir,it->lrt", v_basis[1:], cols(c0b, h * half, half),
            preferred_element_type=F32,
        )
        send = jnp.einsum(
            "lir,it->lrt", v_basis[1:], cols(c0b, (1 - h) * half, half),
            preferred_element_type=F32,
        )
        rest = keep + swap(send, 0, bits)
    own_coefs = []
    for s in range(levels):
        if s == 0:
            mine_b = proj0.astype(BF16)
            theirs_b = swap(mine_b, s, bits)
        else:
            mine_b = rest[0].astype(BF16)
            rest = rest[1:]
            n = rest.shape[0]
            w = mine_b.shape[1] // 2
            parts = [mine_b[:, :w], mine_b[:, w:]]
            if n > 0:
                h = side(s, bits)
                keep = cols(rest, h * w, w)
                send = cols(rest, (1 - h) * w, w)
                parts.append(send.astype(BF16).reshape(n * rank, w))
            payload = jnp.concatenate(parts, axis=0)
            if s < levels - 1:
                payload, m_sib[s] = lax.optimization_barrier((payload, m_sib[s]))
            got = swap(payload, s, bits)
            theirs_b = jnp.concatenate([got[:rank], got[rank : 2 * rank]], axis=1)
            if n > 0:
                recv = got[2 * rank :].reshape(n, rank, w).astype(F32)
                rest = keep + recv
        lower = side(s, bits) == 0
        stacked = jnp.where(
            lower,
            jnp.concatenate([mine_b, theirs_b], axis=0),
            jnp.concatenate([theirs_b, mine_b], axis=0),
        )
        coefs = jnp.dot(coupling[s, 0], stacked, preferred_element_type=F32).astype(BF16)
        own_coefs.append(coefs)
        if s < levels - 1:
            w = coefs.shape[1] // 2
            h = side(s, bits)
            fix = jnp.einsum(
                "nrs,st->nrt", w_own[s], cols(coefs, h * w, w).astype(F32),
                preferred_element_type=F32, precision=lax.Precision.HIGHEST,
            ) + jnp.einsum(
                "nkr,kt->nrt", m_sib[s], cols(stacked, h * w, w).astype(F32),
                preferred_element_type=F32, precision=lax.Precision.HIGHEST,
            )
            rest = rest - fix

    pending = {s: own_coefs[s] for s in range(1, levels)}
    for j in reversed(range(levels - 1)):
        group = [s for s in range(j + 1, levels)]
        joined = gather_half(jnp.stack([pending[s] for s in group]), j, bits)
        for i, s in enumerate(group):
            pending[s] = joined[i]
    full = [own_coefs[0]] + [pending[s] for s in range(1, levels)]
    current = c0
    for s in range(levels):
        current = current - jnp.dot(u_basis[s], full[s], preferred_element_type=F32)
    return current.astype(BF16)


def solution(mesh):
    placed = (
        P(("slab", "wide", "narrow", "inner"), None),
        P(("slab", "wide", "narrow", "inner"), None),
        P(None, ("slab", "wide", "narrow", "inner"), None),
        P(None, ("slab", "wide", "narrow", "inner"), None),
        P(None, ("slab", "wide", "narrow", "inner"), None, None),
    )
    return jax.shard_map(
        on_device,
        mesh=mesh,
        in_specs=placed,
        out_specs=P(("slab", "wide", "narrow", "inner"), None),
        check_vma=False,
    )
```

```python
import jax
import jax.numpy as jnp
from jax import lax
from jax.sharding import PartitionSpec as P

F32 = jnp.float32
BF16 = jnp.bfloat16


def bit_axes():
    bits = []
    for axis in ("inner", "narrow", "wide"):
        for stride in range(lax.axis_size(axis).bit_length() - 1):
            bits.append((axis, stride))
    return bits


def swap(x, bit, bits):
    axis, stride = bits[bit]
    n = lax.axis_size(axis)
    return lax.ppermute(x, axis, [(i, i ^ (1 << stride)) for i in range(n)])


def side(bit, bits):
    axis, stride = bits[bit]
    return (lax.axis_index(axis) >> stride) & 1


def cols(x, start, width):
    return lax.dynamic_slice_in_dim(x, start, width, axis=x.ndim - 1)


def reduce_half(x, bit, bits):
    w = x.shape[-1] // 2
    h = side(bit, bits)
    keep = cols(x, h * w, w)
    send = cols(x, (1 - h) * w, w)
    return keep + swap(send, bit, bits)


def gather_half(x, bit, bits):
    w = x.shape[-1]
    h = side(bit, bits)
    both = jnp.concatenate([x, swap(x, bit, bits), x], axis=-1)
    return cols(both, h * w, 2 * w)


def on_device(templates, leaf_inverse, v_basis, u_basis, coupling):
    bits = bit_axes()
    levels, pixels, rank = v_basis.shape
    width = templates.shape[1]
    c0 = jnp.dot(leaf_inverse, templates, preferred_element_type=F32)
    c0b = c0.astype(BF16)

    mine_c = coupling[:, 0]
    partial = [
        jnp.einsum(
            "lir,is->lrs", v_basis[s + 1:], u_basis[s], preferred_element_type=F32
        ).reshape(-1, rank)
        for s in range(levels - 1)
    ]
    w_own, theirs_c = [None] * levels, []
    for b in range(levels):
        c = mine_c[b]
        parts = [jnp.concatenate([c[:, :rank], c[:, rank:]], axis=0).astype(F32)]
        parts += partial[b:]
        got = swap(jnp.concatenate(parts, axis=0), b, bits)
        theirs = got[: 2 * rank].astype(BF16)
        theirs_c.append(jnp.concatenate([theirs[:rank], theirs[rank:]], axis=1))
        at = 2 * rank
        for s in range(b, levels - 1):
            n = partial[s].shape[0]
            recv = got[at : at + n]
            at += n
            if s == b:
                w_own[s] = jnp.concatenate([partial[s], recv], axis=1)
            else:
                partial[s] = partial[s] + recv
    couple = []
    for s in range(levels):
        lower = side(s, bits) == 0
        mine, theirs = mine_c[s], theirs_c[s]
        first = jnp.concatenate([mine[:, :rank], theirs[:, :rank]], axis=0)
        second = jnp.concatenate([mine[:, rank:], theirs[:, rank:]], axis=0)
        couple.append(
            jnp.concatenate(
                [jnp.where(lower, first, second), jnp.where(lower, second, first)],
                axis=1,
            )
        )

    proj0 = jnp.dot(v_basis[0].T, c0b, preferred_element_type=F32)
    rest = None
    if levels > 1:
        half = width // 2
        h = side(0, bits)
        keep = jnp.einsum(
            "lir,it->lrt", v_basis[1:], cols(c0b, h * half, half),
            preferred_element_type=F32,
        )
        send = jnp.einsum(
            "lir,it->lrt", v_basis[1:], cols(c0b, (1 - h) * half, half),
            preferred_element_type=F32,
        )
        rest = keep + swap(send, 0, bits)
    own_coefs = []
    for s in range(levels):
        if s == 0:
            mine_b = proj0.astype(BF16)
            theirs_b = swap(mine_b, s, bits)
        else:
            mine_b = rest[0].astype(BF16)
            rest = rest[1:]
            n = rest.shape[0]
            w = mine_b.shape[1] // 2
            parts = [mine_b[:, :w], mine_b[:, w:]]
            summed = n == 1 and s == levels - 2
            if summed:
                last = rest[0].astype(BF16)
                parts += [last[:, :w], last[:, w:]]
            elif n > 0:
                h = side(s, bits)
                keep = cols(rest, h * w, w)
                send = cols(rest, (1 - h) * w, w)
                parts.append(send.astype(BF16).reshape(n * rank, w))
            got = swap(jnp.concatenate(parts, axis=0), s, bits)
            theirs_b = jnp.concatenate([got[:rank], got[rank : 2 * rank]], axis=1)
            if summed:
                recv = jnp.concatenate([got[2 * rank : 3 * rank], got[3 * rank :]], axis=1)
                rest = rest + recv.astype(F32)[None]
            elif n > 0:
                recv = got[2 * rank :].reshape(n, rank, w).astype(F32)
                rest = keep + recv
        stacked = jnp.concatenate([mine_b, theirs_b], axis=0)
        coefs = jnp.dot(couple[s], stacked, preferred_element_type=F32).astype(BF16)
        own_coefs.append(coefs[:rank])
        if s < levels - 1:
            w = coefs.shape[1] // 2
            if rest.shape[-1] == coefs.shape[1]:
                piece = coefs.astype(F32)
            else:
                piece = cols(coefs, side(s, bits) * w, w).astype(F32)
            fix = jnp.dot(
                w_own[s], piece, preferred_element_type=F32,
                precision=lax.Precision.HIGHEST,
            )
            rest = rest - fix.reshape(rest.shape)

    full = [own_coefs[0]] + [None] * (levels - 1)
    pending = {s: own_coefs[s] for s in range(1, levels)}
    top = {s: s - 1 for s in range(1, levels)}
    if levels > 2:
        top[levels - 1] = levels - 3
    for j in reversed(range(levels - 1)):
        group = [s for s in range(1, levels) if top[s] >= j]
        if not group:
            continue
        joined = gather_half(jnp.stack([pending[s] for s in group]), j, bits)
        for i, s in enumerate(group):
            pending[s] = joined[i]
    for s in range(1, levels):
        full[s] = pending[s]
    current = c0
    for s in range(levels):
        current = current - jnp.dot(u_basis[s], full[s], preferred_element_type=F32)
    return current.astype(BF16)


def solution(mesh):
    placed = (
        P(("slab", "wide", "narrow", "inner"), None),
        P(("slab", "wide", "narrow", "inner"), None),
        P(None, ("slab", "wide", "narrow", "inner"), None),
        P(None, ("slab", "wide", "narrow", "inner"), None),
        P(None, ("slab", "wide", "narrow", "inner"), None, None),
    )
    return jax.shard_map(
        on_device,
        mesh=mesh,
        in_specs=placed,
        out_specs=P(("slab", "wide", "narrow", "inner"), None),
        check_vma=False,
    )
```

```python
import jax
import jax.numpy as jnp
from jax import lax
from jax.sharding import PartitionSpec as P

F32 = jnp.float32
BF16 = jnp.bfloat16


def bit_axes():
    bits = []
    for axis in ("inner", "narrow", "wide"):
        for stride in range(lax.axis_size(axis).bit_length() - 1):
            bits.append((axis, stride))
    return bits


def swap(x, bit, bits):
    axis, stride = bits[bit]
    n = lax.axis_size(axis)
    return lax.ppermute(x, axis, [(i, i ^ (1 << stride)) for i in range(n)])


def side(bit, bits):
    axis, stride = bits[bit]
    return (lax.axis_index(axis) >> stride) & 1


def cols(x, start, width):
    return lax.dynamic_slice_in_dim(x, start, width, axis=x.ndim - 1)


def reduce_half(x, bit, bits):
    w = x.shape[-1] // 2
    h = side(bit, bits)
    keep = cols(x, h * w, w)
    send = cols(x, (1 - h) * w, w)
    return keep + swap(send, bit, bits)


def gather_half(x, bit, bits):
    w = x.shape[-1]
    h = side(bit, bits)
    both = jnp.concatenate([x, swap(x, bit, bits), x], axis=-1)
    return cols(both, h * w, 2 * w)


def on_device(templates, leaf_inverse, v_basis, u_basis, coupling):
    bits = bit_axes()
    levels, pixels, rank = v_basis.shape
    width = templates.shape[1]
    cross = jnp.einsum("kis,lir->klrs", u_basis, v_basis, preferred_element_type=F32)
    counts = [levels - 1 - k for k in range(levels - 1)]
    suffix = jnp.concatenate(
        [cross[k, k + 1 :].reshape(-1, rank) for k in range(levels - 1)], axis=0
    )
    w_own, w_sib, sent = [None] * levels, [None] * levels, [None] * levels
    for b in range(levels - 1):
        n = counts[b] * rank
        if b == 0:
            suffix, templates = lax.optimization_barrier((suffix, templates))
        sent[b] = suffix
        got = swap(suffix, b, bits)
        w_own[b] = suffix[:n].reshape(counts[b], rank, rank)
        w_sib[b] = got[:n].reshape(counts[b], rank, rank)
        suffix = suffix[n:] + got[n:]
    couple_sib = [swap(coupling[s, 0], s, bits) for s in range(levels)]

    c0 = jnp.dot(leaf_inverse, templates, preferred_element_type=F32)
    c0b = c0.astype(BF16)
    proj0 = jnp.dot(v_basis[0].T, c0b, preferred_element_type=F32)
    rest = None
    if levels > 1:
        half = width // 2
        h = side(0, bits)
        keep = jnp.einsum(
            "lir,it->lrt", v_basis[1:], cols(c0b, h * half, half),
            preferred_element_type=F32,
        )
        send = jnp.einsum(
            "lir,it->lrt", v_basis[1:], cols(c0b, (1 - h) * half, half),
            preferred_element_type=F32,
        )
        rest = keep + swap(send, 0, bits)
    own_coefs = []
    for s in range(levels):
        if s == 0:
            mine_b = proj0.astype(BF16)
            theirs_b = swap(mine_b, s, bits)
        else:
            mine_b = rest[0].astype(BF16)
            rest = rest[1:]
            n = rest.shape[0]
            w = mine_b.shape[1] // 2
            parts = [mine_b[:, :w], mine_b[:, w:]]
            summed = n == 1 and s == levels - 2
            if summed:
                last = rest[0].astype(BF16)
                parts += [last[:, :w], last[:, w:]]
            elif n > 0:
                h = side(s, bits)
                keep = cols(rest, h * w, w)
                send = cols(rest, (1 - h) * w, w)
                parts.append(send.astype(BF16).reshape(n * rank, w))
            payload = jnp.concatenate(parts, axis=0)
            if s < levels - 1:
                payload, w_sib[s] = lax.optimization_barrier((payload, w_sib[s]))
            got = swap(payload, s, bits)
            theirs_b = jnp.concatenate([got[:rank], got[rank : 2 * rank]], axis=1)
            if summed:
                recv = jnp.concatenate([got[2 * rank : 3 * rank], got[3 * rank :]], axis=1)
                rest = rest + recv.astype(F32)[None]
            elif n > 0:
                recv = got[2 * rank :].reshape(n, rank, w).astype(F32)
                rest = keep + recv
        lower = side(s, bits) == 0
        stacked = jnp.where(
            lower,
            jnp.concatenate([mine_b, theirs_b], axis=0),
            jnp.concatenate([theirs_b, mine_b], axis=0),
        )
        if s == 0 and levels > 2:
            stacked, sent[1] = lax.optimization_barrier((stacked, sent[1]))
        coefs = jnp.dot(coupling[s, 0], stacked, preferred_element_type=F32).astype(BF16)
        own_coefs.append(coefs)
        if s < levels - 1:
            sib = jnp.dot(couple_sib[s], stacked, preferred_element_type=F32).astype(BF16)
            w = coefs.shape[1] // 2
            if rest.shape[-1] == coefs.shape[1]:
                co, cs = coefs, sib
            else:
                h = side(s, bits)
                co, cs = cols(coefs, h * w, w), cols(sib, h * w, w)
            fix = jnp.einsum(
                "nrs,st->nrt", w_own[s], co.astype(F32),
                preferred_element_type=F32, precision=lax.Precision.HIGHEST,
            ) + jnp.einsum(
                "nrs,st->nrt", w_sib[s], cs.astype(F32),
                preferred_element_type=F32, precision=lax.Precision.HIGHEST,
            )
            rest = rest - fix.reshape(rest.shape)

    full = [own_coefs[0]] + [None] * (levels - 1)
    pending = {s: own_coefs[s] for s in range(1, levels)}
    top = {s: s - 1 for s in range(1, levels)}
    if levels > 2:
        top[levels - 1] = levels - 3
    for j in reversed(range(levels - 1)):
        group = [s for s in range(1, levels) if top[s] >= j]
        if not group:
            continue
        joined = gather_half(jnp.stack([pending[s] for s in group]), j, bits)
        for i, s in enumerate(group):
            pending[s] = joined[i]
    for s in range(1, levels):
        full[s] = pending[s]
    current = c0
    for s in range(levels):
        current = current - jnp.dot(u_basis[s], full[s], preferred_element_type=F32)
    return current.astype(BF16)


def solution(mesh):
    placed = (
        P(("slab", "wide", "narrow", "inner"), None),
        P(("slab", "wide", "narrow", "inner"), None),
        P(None, ("slab", "wide", "narrow", "inner"), None),
        P(None, ("slab", "wide", "narrow", "inner"), None),
        P(None, ("slab", "wide", "narrow", "inner"), None, None),
    )
    return jax.shard_map(
        on_device,
        mesh=mesh,
        in_specs=placed,
        out_specs=P(("slab", "wide", "narrow", "inner"), None),
        check_vma=False,
    )
```

```python
import jax
import jax.numpy as jnp
from jax import lax
from jax.sharding import PartitionSpec as P

F32 = jnp.float32
BF16 = jnp.bfloat16


def bit_axes():
    bits = []
    for axis in ("inner", "narrow", "wide"):
        for stride in range(lax.axis_size(axis).bit_length() - 1):
            bits.append((axis, stride))
    return bits


def swap(x, bit, bits):
    axis, stride = bits[bit]
    n = lax.axis_size(axis)
    return lax.ppermute(x, axis, [(i, i ^ (1 << stride)) for i in range(n)])


def side(bit, bits):
    axis, stride = bits[bit]
    return (lax.axis_index(axis) >> stride) & 1


def cols(x, start, width):
    return lax.dynamic_slice_in_dim(x, start, width, axis=x.ndim - 1)


def reduce_half(x, bit, bits):
    w = x.shape[-1] // 2
    h = side(bit, bits)
    keep = cols(x, h * w, w)
    send = cols(x, (1 - h) * w, w)
    return keep + swap(send, bit, bits)


def gather_half(x, bit, bits):
    w = x.shape[-1]
    h = side(bit, bits)
    both = jnp.concatenate([x, swap(x, bit, bits), x], axis=-1)
    return cols(both, h * w, 2 * w)


def on_device(templates, leaf_inverse, v_basis, u_basis, coupling):
    bits = bit_axes()
    levels, pixels, rank = v_basis.shape
    width = templates.shape[1]
    c0 = jnp.dot(leaf_inverse, templates, preferred_element_type=F32)
    c0b = c0.astype(BF16)

    mine_c = coupling[:, 0]
    partial = [
        jnp.einsum(
            "lir,is->lrs", v_basis[s + 1:], u_basis[s], preferred_element_type=F32
        ).reshape(-1, rank)
        for s in range(levels - 1)
    ]
    w_own, theirs_c = [None] * levels, []
    for b in range(levels):
        c = mine_c[b]
        parts = [jnp.concatenate([c[:, :rank], c[:, rank:]], axis=0).astype(F32)]
        parts += partial[b:]
        got = swap(jnp.concatenate(parts, axis=0), b, bits)
        theirs = got[: 2 * rank].astype(BF16)
        theirs_c.append(jnp.concatenate([theirs[:rank], theirs[rank:]], axis=1))
        at = 2 * rank
        for s in range(b, levels - 1):
            n = partial[s].shape[0]
            recv = got[at : at + n]
            at += n
            if s == b:
                w_own[s] = jnp.concatenate([partial[s], recv], axis=1)
            else:
                partial[s] = partial[s] + recv
    couple = []
    for s in range(levels):
        lower = side(s, bits) == 0
        mine, theirs = mine_c[s], theirs_c[s]
        first = jnp.concatenate([mine[:, :rank], theirs[:, :rank]], axis=0)
        second = jnp.concatenate([mine[:, rank:], theirs[:, rank:]], axis=0)
        couple.append(
            jnp.concatenate(
                [jnp.where(lower, first, second), jnp.where(lower, second, first)],
                axis=1,
            )
        )

    proj0 = jnp.dot(v_basis[0].T, c0b, preferred_element_type=F32)
    rest = None
    if levels > 1:
        half = width // 2
        h = side(0, bits)
        keep = jnp.einsum(
            "lir,it->lrt", v_basis[1:], cols(c0b, h * half, half),
            preferred_element_type=F32,
        )
        send = jnp.einsum(
            "lir,it->lrt", v_basis[1:], cols(c0b, (1 - h) * half, half),
            preferred_element_type=F32,
        )
        rest = keep + swap(send, 0, bits)
    own_coefs = []
    for s in range(levels):
        if s == 0:
            mine_b = proj0.astype(BF16)
            theirs_b = swap(mine_b, s, bits)
        else:
            mine_b = rest[0].astype(BF16)
            rest = rest[1:]
            n = rest.shape[0]
            w = mine_b.shape[1] // 2
            parts = [mine_b[:, :w], mine_b[:, w:]]
            summed = n == 1 and s == levels - 2
            if summed:
                last = rest[0].astype(BF16)
                parts += [last[:, :w], last[:, w:]]
            elif n > 0:
                h = side(s, bits)
                keep = cols(rest, h * w, w)
                send = cols(rest, (1 - h) * w, w)
                parts.append(send.astype(BF16).reshape(n * rank, w))
            got = swap(jnp.concatenate(parts, axis=0), s, bits)
            theirs_b = jnp.concatenate([got[:rank], got[rank : 2 * rank]], axis=1)
            if summed:
                recv = jnp.concatenate([got[2 * rank : 3 * rank], got[3 * rank :]], axis=1)
                rest = rest + recv.astype(F32)[None]
            elif n > 0:
                recv = got[2 * rank :].reshape(n, rank, w).astype(F32)
                rest = keep + recv
        stacked = jnp.concatenate([mine_b, theirs_b], axis=0)
        coefs = jnp.dot(couple[s], stacked, preferred_element_type=F32).astype(BF16)
        own_coefs.append(coefs[:rank])
        if s < levels - 1:
            w = coefs.shape[1] // 2
            if rest.shape[-1] == coefs.shape[1]:
                piece = coefs.astype(F32)
            else:
                piece = cols(coefs, side(s, bits) * w, w).astype(F32)
            fix = jnp.dot(
                w_own[s], piece, preferred_element_type=F32,
                precision=lax.Precision.HIGHEST,
            )
            rest = rest - fix.reshape(rest.shape)

    full = [own_coefs[0]] + [None] * (levels - 1)
    pending = {s: own_coefs[s] for s in range(1, levels)}
    top = {s: s - 1 for s in range(1, levels)}
    if levels > 2:
        top[levels - 1] = levels - 3
    early = c0 - jnp.dot(u_basis[0], own_coefs[0], preferred_element_type=F32)
    joined = None
    for j in reversed(range(levels - 1)):
        group = [s for s in range(1, levels) if top[s] >= j]
        if not group:
            continue
        joined = gather_half(jnp.stack([pending[s] for s in group]), j, bits)
        for i, s in enumerate(group):
            pending[s] = joined[i]
    if joined is None:
        joined = jnp.stack([pending[s] for s in range(1, levels)])
    current = early - jnp.einsum(
        "lir,lrt->it", u_basis[1:], joined, preferred_element_type=F32
    )
    return current.astype(BF16)


def solution(mesh):
    placed = (
        P(("slab", "wide", "narrow", "inner"), None),
        P(("slab", "wide", "narrow", "inner"), None),
        P(None, ("slab", "wide", "narrow", "inner"), None),
        P(None, ("slab", "wide", "narrow", "inner"), None),
        P(None, ("slab", "wide", "narrow", "inner"), None, None),
    )
    return jax.shard_map(
        on_device,
        mesh=mesh,
        in_specs=placed,
        out_specs=P(("slab", "wide", "narrow", "inner"), None),
        check_vma=False,
    )
```

```python
import jax
import jax.numpy as jnp
from jax import lax
from jax.sharding import PartitionSpec as P

F32 = jnp.float32
BF16 = jnp.bfloat16


def bit_axes():
    bits = []
    for axis in ("inner", "narrow", "wide"):
        for stride in range(lax.axis_size(axis).bit_length() - 1):
            bits.append((axis, stride))
    return bits


def swap(x, bit, bits):
    axis, stride = bits[bit]
    n = lax.axis_size(axis)
    return lax.ppermute(x, axis, [(i, i ^ (1 << stride)) for i in range(n)])


def side(bit, bits):
    axis, stride = bits[bit]
    return (lax.axis_index(axis) >> stride) & 1


def cols(x, start, width):
    return lax.dynamic_slice_in_dim(x, start, width, axis=x.ndim - 1)


def reduce_half(x, bit, bits):
    w = x.shape[-1] // 2
    h = side(bit, bits)
    keep = cols(x, h * w, w)
    send = cols(x, (1 - h) * w, w)
    return keep + swap(send, bit, bits)


def gather_half(x, bit, bits):
    w = x.shape[-1]
    h = side(bit, bits)
    both = jnp.concatenate([x, swap(x, bit, bits), x], axis=-1)
    return cols(both, h * w, 2 * w)


def on_device(templates, leaf_inverse, v_basis, u_basis, coupling):
    bits = bit_axes()
    levels, pixels, rank = v_basis.shape
    width = templates.shape[1]
    c0 = jnp.dot(leaf_inverse, templates, preferred_element_type=F32)

    mine_c = coupling[:, 0]
    partial = [
        jnp.einsum(
            "lir,is->lrs", v_basis[s + 1:], u_basis[s], preferred_element_type=F32
        ).reshape(-1, rank)
        for s in range(levels - 1)
    ]
    w_own, theirs_c = [None] * levels, []
    for b in range(levels):
        c = mine_c[b]
        parts = [jnp.concatenate([c[:, :rank], c[:, rank:]], axis=0).astype(F32)]
        parts += partial[b:]
        got = swap(jnp.concatenate(parts, axis=0), b, bits)
        theirs = got[: 2 * rank].astype(BF16)
        theirs_c.append(jnp.concatenate([theirs[:rank], theirs[rank:]], axis=1))
        at = 2 * rank
        for s in range(b, levels - 1):
            n = partial[s].shape[0]
            recv = got[at : at + n]
            at += n
            if s == b:
                w_own[s] = jnp.concatenate([partial[s], recv], axis=1)
            else:
                partial[s] = partial[s] + recv
    couple = []
    for s in range(levels):
        lower = side(s, bits) == 0
        mine, theirs = mine_c[s], theirs_c[s]
        first = jnp.concatenate([mine[:, :rank], theirs[:, :rank]], axis=0)
        second = jnp.concatenate([mine[:, rank:], theirs[:, rank:]], axis=0)
        couple.append(
            jnp.concatenate(
                [jnp.where(lower, first, second), jnp.where(lower, second, first)],
                axis=1,
            )
        )

    vl = jnp.einsum("lir,ij->lrj", v_basis, leaf_inverse, preferred_element_type=F32)
    vl_hi = vl.astype(BF16)
    vl_lo = (vl - vl_hi.astype(F32)).astype(BF16)

    def project(lv, x):
        return jnp.einsum(
            "lrj,jt->lrt", vl_hi[lv], x, preferred_element_type=F32
        ) + jnp.einsum("lrj,jt->lrt", vl_lo[lv], x, preferred_element_type=F32)

    proj0 = project(slice(0, 1), templates)[0]
    rest = None
    if levels > 1:
        half = width // 2
        h = side(0, bits)
        keep = project(slice(1, levels), cols(templates, h * half, half))
        send = project(slice(1, levels), cols(templates, (1 - h) * half, half))
        rest = keep + swap(send, 0, bits)
    own_coefs = []
    for s in range(levels):
        if s == 0:
            mine_b = proj0.astype(BF16)
            theirs_b = swap(mine_b, s, bits)
        else:
            mine_b = rest[0].astype(BF16)
            rest = rest[1:]
            n = rest.shape[0]
            w = mine_b.shape[1] // 2
            parts = [mine_b[:, :w], mine_b[:, w:]]
            summed = n == 1 and s == levels - 2
            if summed:
                last = rest[0].astype(BF16)
                parts += [last[:, :w], last[:, w:]]
            elif n > 0:
                h = side(s, bits)
                keep = cols(rest, h * w, w)
                send = cols(rest, (1 - h) * w, w)
                parts.append(send.astype(BF16).reshape(n * rank, w))
            got = swap(jnp.concatenate(parts, axis=0), s, bits)
            theirs_b = jnp.concatenate([got[:rank], got[rank : 2 * rank]], axis=1)
            if summed:
                recv = jnp.concatenate([got[2 * rank : 3 * rank], got[3 * rank :]], axis=1)
                rest = rest + recv.astype(F32)[None]
            elif n > 0:
                recv = got[2 * rank :].reshape(n, rank, w).astype(F32)
                rest = keep + recv
        stacked = jnp.concatenate([mine_b, theirs_b], axis=0)
        coefs = jnp.dot(couple[s], stacked, preferred_element_type=F32).astype(BF16)
        own_coefs.append(coefs[:rank])
        if s < levels - 1:
            w = coefs.shape[1] // 2
            if rest.shape[-1] == coefs.shape[1]:
                piece = coefs.astype(F32)
            else:
                piece = cols(coefs, side(s, bits) * w, w).astype(F32)
            fix = jnp.dot(
                w_own[s], piece, preferred_element_type=F32,
                precision=lax.Precision.HIGHEST,
            )
            rest = rest - fix.reshape(rest.shape)

    full = [own_coefs[0]] + [None] * (levels - 1)
    pending = {s: own_coefs[s] for s in range(1, levels)}
    top = {s: s - 1 for s in range(1, levels)}
    if levels > 2:
        top[levels - 1] = levels - 3
    for j in reversed(range(levels - 1)):
        group = [s for s in range(1, levels) if top[s] >= j]
        if not group:
            continue
        joined = gather_half(jnp.stack([pending[s] for s in group]), j, bits)
        for i, s in enumerate(group):
            pending[s] = joined[i]
    for s in range(1, levels):
        full[s] = pending[s]
    current = c0
    for s in range(levels):
        current = current - jnp.dot(u_basis[s], full[s], preferred_element_type=F32)
    return current.astype(BF16)


def solution(mesh):
    placed = (
        P(("slab", "wide", "narrow", "inner"), None),
        P(("slab", "wide", "narrow", "inner"), None),
        P(None, ("slab", "wide", "narrow", "inner"), None),
        P(None, ("slab", "wide", "narrow", "inner"), None),
        P(None, ("slab", "wide", "narrow", "inner"), None, None),
    )
    return jax.shard_map(
        on_device,
        mesh=mesh,
        in_specs=placed,
        out_specs=P(("slab", "wide", "narrow", "inner"), None),
        check_vma=False,
    )
```

```python
import jax
import jax.numpy as jnp
from jax import lax
from jax.sharding import PartitionSpec as P

F32 = jnp.float32
BF16 = jnp.bfloat16


def bit_axes():
    bits = []
    for axis in ("inner", "narrow", "wide"):
        for stride in range(lax.axis_size(axis).bit_length() - 1):
            bits.append((axis, stride))
    return bits


def swap(x, bit, bits):
    axis, stride = bits[bit]
    n = lax.axis_size(axis)
    return lax.ppermute(x, axis, [(i, i ^ (1 << stride)) for i in range(n)])


def side(bit, bits):
    axis, stride = bits[bit]
    return (lax.axis_index(axis) >> stride) & 1


def cols(x, start, width):
    return lax.dynamic_slice_in_dim(x, start, width, axis=x.ndim - 1)


def reduce_half(x, bit, bits):
    w = x.shape[-1] // 2
    h = side(bit, bits)
    keep = cols(x, h * w, w)
    send = cols(x, (1 - h) * w, w)
    return keep + swap(send, bit, bits)


def gather_half(x, bit, bits):
    w = x.shape[-1]
    h = side(bit, bits)
    both = jnp.concatenate([x, swap(x, bit, bits), x], axis=-1)
    return cols(both, h * w, 2 * w)


def on_device(templates, leaf_inverse, v_basis, u_basis, coupling):
    bits = bit_axes()
    levels, pixels, rank = v_basis.shape
    width = templates.shape[1]
    c0 = jnp.dot(leaf_inverse, templates, preferred_element_type=F32)

    cross = jnp.einsum("kis,lir->klrs", u_basis, v_basis, preferred_element_type=F32)
    counts = [levels - 1 - k for k in range(levels - 1)]
    suffix = jnp.concatenate(
        [cross[k, k + 1 :].reshape(-1, rank) for k in range(levels - 1)], axis=0
    )
    w_own, w_sib = [None] * levels, [None] * levels
    for b in range(levels - 1):
        n = counts[b] * rank
        got = swap(suffix, b, bits)
        w_own[b] = suffix[:n].reshape(counts[b], rank, rank)
        w_sib[b] = got[:n].reshape(counts[b], rank, rank)
        suffix = suffix[n:] + got[n:]
    couple_sib = [swap(coupling[s, 0], s, bits) for s in range(levels - 1)]

    vl = jnp.einsum("lir,ij->lrj", v_basis, leaf_inverse, preferred_element_type=F32)
    vl_hi = vl.astype(BF16)
    vl_lo = (vl - vl_hi.astype(F32)).astype(BF16)

    def project(lv, x):
        return jnp.einsum(
            "lrj,jt->lrt", vl_hi[lv], x, preferred_element_type=F32
        ) + jnp.einsum("lrj,jt->lrt", vl_lo[lv], x, preferred_element_type=F32)

    proj0 = project(slice(0, 1), templates)[0]
    rest = None
    if levels > 1:
        half = width // 2
        h = side(0, bits)
        keep = project(slice(1, levels), cols(templates, h * half, half))
        send = project(slice(1, levels), cols(templates, (1 - h) * half, half))
        rest = keep + swap(send, 0, bits)
    own_coefs = []
    for s in range(levels):
        if s == 0:
            mine_b = proj0.astype(BF16)
            theirs_b = swap(mine_b, s, bits)
        else:
            mine_b = rest[0].astype(BF16)
            rest = rest[1:]
            n = rest.shape[0]
            w = mine_b.shape[1] // 2
            parts = [mine_b[:, :w], mine_b[:, w:]]
            summed = n == 1 and s == levels - 2
            if summed:
                last = rest[0].astype(BF16)
                parts += [last[:, :w], last[:, w:]]
            elif n > 0:
                h = side(s, bits)
                keep = cols(rest, h * w, w)
                send = cols(rest, (1 - h) * w, w)
                parts.append(send.astype(BF16).reshape(n * rank, w))
            payload = jnp.concatenate(parts, axis=0)
            if s < levels - 1:
                payload, w_sib[s] = lax.optimization_barrier((payload, w_sib[s]))
            got = swap(payload, s, bits)
            theirs_b = jnp.concatenate([got[:rank], got[rank : 2 * rank]], axis=1)
            if summed:
                recv = jnp.concatenate([got[2 * rank : 3 * rank], got[3 * rank :]], axis=1)
                rest = rest + recv.astype(F32)[None]
            elif n > 0:
                recv = got[2 * rank :].reshape(n, rank, w).astype(F32)
                rest = keep + recv
        lower = side(s, bits) == 0
        stacked = jnp.where(
            lower,
            jnp.concatenate([mine_b, theirs_b], axis=0),
            jnp.concatenate([theirs_b, mine_b], axis=0),
        )
        if s == 0:
            stacked, couple_sib = lax.optimization_barrier((stacked, couple_sib))
        coefs = jnp.dot(coupling[s, 0], stacked, preferred_element_type=F32).astype(BF16)
        own_coefs.append(coefs)
        if s < levels - 1:
            sib = jnp.dot(couple_sib[s], stacked, preferred_element_type=F32).astype(BF16)
            w = coefs.shape[1] // 2
            if rest.shape[-1] == coefs.shape[1]:
                co, cs = coefs, sib
            else:
                h = side(s, bits)
                co, cs = cols(coefs, h * w, w), cols(sib, h * w, w)
            fix = jnp.einsum(
                "nrs,st->nrt", w_own[s], co.astype(F32),
                preferred_element_type=F32, precision=lax.Precision.HIGHEST,
            ) + jnp.einsum(
                "nrs,st->nrt", w_sib[s], cs.astype(F32),
                preferred_element_type=F32, precision=lax.Precision.HIGHEST,
            )
            rest = rest - fix.reshape(rest.shape)

    full = [own_coefs[0]] + [None] * (levels - 1)
    pending = {s: own_coefs[s] for s in range(1, levels)}
    top = {s: s - 1 for s in range(1, levels)}
    if levels > 2:
        top[levels - 1] = levels - 3
    for j in reversed(range(levels - 1)):
        group = [s for s in range(1, levels) if top[s] >= j]
        if not group:
            continue
        joined = gather_half(jnp.stack([pending[s] for s in group]), j, bits)
        for i, s in enumerate(group):
            pending[s] = joined[i]
    for s in range(1, levels):
        full[s] = pending[s]
    current = c0
    for s in range(levels):
        current = current - jnp.dot(u_basis[s], full[s], preferred_element_type=F32)
    return current.astype(BF16)


def solution(mesh):
    placed = (
        P(("slab", "wide", "narrow", "inner"), None),
        P(("slab", "wide", "narrow", "inner"), None),
        P(None, ("slab", "wide", "narrow", "inner"), None),
        P(None, ("slab", "wide", "narrow", "inner"), None),
        P(None, ("slab", "wide", "narrow", "inner"), None, None),
    )
    return jax.shard_map(
        on_device,
        mesh=mesh,
        in_specs=placed,
        out_specs=P(("slab", "wide", "narrow", "inner"), None),
        check_vma=False,
    )
```

```python
import jax
import jax.numpy as jnp
from jax import lax
from jax.sharding import PartitionSpec as P

F32 = jnp.float32
BF16 = jnp.bfloat16


def bit_axes():
    bits = []
    for axis in ("inner", "narrow", "wide"):
        for stride in range(lax.axis_size(axis).bit_length() - 1):
            bits.append((axis, stride))
    return bits


def swap(x, bit, bits):
    axis, stride = bits[bit]
    n = lax.axis_size(axis)
    return lax.ppermute(x, axis, [(i, i ^ (1 << stride)) for i in range(n)])


def side(bit, bits):
    axis, stride = bits[bit]
    return (lax.axis_index(axis) >> stride) & 1


def cols(x, start, width):
    return lax.dynamic_slice_in_dim(x, start, width, axis=x.ndim - 1)


def reduce_half(x, bit, bits):
    w = x.shape[-1] // 2
    h = side(bit, bits)
    keep = cols(x, h * w, w)
    send = cols(x, (1 - h) * w, w)
    return keep + swap(send, bit, bits)


def gather_half(x, bit, bits):
    w = x.shape[-1]
    h = side(bit, bits)
    both = jnp.concatenate([x, swap(x, bit, bits), x], axis=-1)
    return cols(both, h * w, 2 * w)


def on_device(templates, leaf_inverse, v_basis, u_basis, coupling):
    bits = bit_axes()
    levels, pixels, rank = v_basis.shape
    width = templates.shape[1]
    c0 = jnp.dot(leaf_inverse, templates, preferred_element_type=F32)

    mine_c = coupling[:, 0]
    partial = [
        jnp.einsum(
            "lir,is->lrs", v_basis[s + 1:], u_basis[s], preferred_element_type=F32
        ).reshape(-1, rank)
        for s in range(levels - 1)
    ]
    w_own, theirs_c = [None] * levels, []
    for b in range(levels):
        c = mine_c[b]
        parts = [jnp.concatenate([c[:, :rank], c[:, rank:]], axis=0).astype(F32)]
        parts += partial[b:]
        got = swap(jnp.concatenate(parts, axis=0), b, bits)
        theirs = got[: 2 * rank].astype(BF16)
        theirs_c.append(jnp.concatenate([theirs[:rank], theirs[rank:]], axis=1))
        at = 2 * rank
        for s in range(b, levels - 1):
            n = partial[s].shape[0]
            recv = got[at : at + n]
            at += n
            if s == b:
                w_own[s] = jnp.concatenate([partial[s], recv], axis=1)
            else:
                partial[s] = partial[s] + recv
    couple = []
    for s in range(levels):
        lower = side(s, bits) == 0
        mine, theirs = mine_c[s], theirs_c[s]
        first = jnp.concatenate([mine[:, :rank], theirs[:, :rank]], axis=0)
        second = jnp.concatenate([mine[:, rank:], theirs[:, rank:]], axis=0)
        couple.append(
            jnp.concatenate(
                [jnp.where(lower, first, second), jnp.where(lower, second, first)],
                axis=1,
            )
        )

    vl = jnp.einsum("lir,ij->lrj", v_basis, leaf_inverse, preferred_element_type=F32)
    vl_hi = vl.astype(BF16)
    vl_lo = (vl - vl_hi.astype(F32)).astype(BF16)

    def project(lv, x):
        return jnp.einsum(
            "lrj,jt->lrt", vl_hi[lv], x, preferred_element_type=F32
        ) + jnp.einsum("lrj,jt->lrt", vl_lo[lv], x, preferred_element_type=F32)

    proj0 = project(slice(0, 1), templates)[0].astype(BF16)
    rest = None
    half = width // 2
    if levels > 1:
        h = side(0, bits)
        keep = project(slice(1, levels), cols(templates, h * half, half))
        send = project(slice(1, levels), cols(templates, (1 - h) * half, half))
        got0 = swap(
            jnp.concatenate(
                [proj0[:, :half], proj0[:, half:],
                 send.astype(BF16).reshape((levels - 1) * rank, half)],
                axis=0,
            ),
            0,
            bits,
        )
        theirs0 = jnp.concatenate([got0[:rank], got0[rank : 2 * rank]], axis=1)
        rest = keep + got0[2 * rank :].reshape(levels - 1, rank, half).astype(F32)
    else:
        theirs0 = swap(proj0, 0, bits)
    own_coefs = []
    for s in range(levels):
        if s == 0:
            mine_b, theirs_b = proj0, theirs0
        else:
            mine_b = rest[0].astype(BF16)
            rest = rest[1:]
            n = rest.shape[0]
            w = mine_b.shape[1] // 2
            parts = [mine_b[:, :w], mine_b[:, w:]]
            summed = n == 1 and s == levels - 2
            if summed:
                last = rest[0].astype(BF16)
                parts += [last[:, :w], last[:, w:]]
            elif n > 0:
                h = side(s, bits)
                keep = cols(rest, h * w, w)
                send = cols(rest, (1 - h) * w, w)
                parts.append(send.astype(BF16).reshape(n * rank, w))
            got = swap(jnp.concatenate(parts, axis=0), s, bits)
            theirs_b = jnp.concatenate([got[:rank], got[rank : 2 * rank]], axis=1)
            if summed:
                recv = jnp.concatenate([got[2 * rank : 3 * rank], got[3 * rank :]], axis=1)
                rest = rest + recv.astype(F32)[None]
            elif n > 0:
                recv = got[2 * rank :].reshape(n, rank, w).astype(F32)
                rest = keep + recv
        stacked = jnp.concatenate([mine_b, theirs_b], axis=0)
        coefs = jnp.dot(couple[s], stacked, preferred_element_type=F32).astype(BF16)
        own_coefs.append(coefs[:rank])
        if s < levels - 1:
            w = coefs.shape[1] // 2
            if rest.shape[-1] == coefs.shape[1]:
                piece = coefs.astype(F32)
            else:
                piece = cols(coefs, side(s, bits) * w, w).astype(F32)
            fix = jnp.dot(
                w_own[s], piece, preferred_element_type=F32,
                precision=lax.Precision.HIGHEST,
            )
            rest = rest - fix.reshape(rest.shape)

    full = [own_coefs[0]] + [None] * (levels - 1)
    pending = {s: own_coefs[s] for s in range(1, levels)}
    top = {s: s - 1 for s in range(1, levels)}
    if levels > 2:
        top[levels - 1] = levels - 3
    for j in reversed(range(levels - 1)):
        group = [s for s in range(1, levels) if top[s] >= j]
        if not group:
            continue
        joined = gather_half(jnp.stack([pending[s] for s in group]), j, bits)
        for i, s in enumerate(group):
            pending[s] = joined[i]
    for s in range(1, levels):
        full[s] = pending[s]
    current = c0
    for s in range(levels):
        current = current - jnp.dot(u_basis[s], full[s], preferred_element_type=F32)
    return current.astype(BF16)


def solution(mesh):
    placed = (
        P(("slab", "wide", "narrow", "inner"), None),
        P(("slab", "wide", "narrow", "inner"), None),
        P(None, ("slab", "wide", "narrow", "inner"), None),
        P(None, ("slab", "wide", "narrow", "inner"), None),
        P(None, ("slab", "wide", "narrow", "inner"), None, None),
    )
    return jax.shard_map(
        on_device,
        mesh=mesh,
        in_specs=placed,
        out_specs=P(("slab", "wide", "narrow", "inner"), None),
        check_vma=False,
    )
```

```python
import jax
import jax.numpy as jnp
from jax import lax
from jax.sharding import PartitionSpec as P

F32 = jnp.float32
BF16 = jnp.bfloat16


def bit_axes():
    bits = []
    for axis in ("inner", "narrow", "wide"):
        for stride in range(lax.axis_size(axis).bit_length() - 1):
            bits.append((axis, stride))
    return bits


def swap(x, bit, bits):
    axis, stride = bits[bit]
    n = lax.axis_size(axis)
    return lax.ppermute(x, axis, [(i, i ^ (1 << stride)) for i in range(n)])


def side(bit, bits):
    axis, stride = bits[bit]
    return (lax.axis_index(axis) >> stride) & 1


def cols(x, start, width):
    return lax.dynamic_slice_in_dim(x, start, width, axis=x.ndim - 1)


def reduce_half(x, bit, bits):
    w = x.shape[-1] // 2
    h = side(bit, bits)
    keep = cols(x, h * w, w)
    send = cols(x, (1 - h) * w, w)
    return keep + swap(send, bit, bits)


def gather_half(x, bit, bits):
    w = x.shape[-1]
    h = side(bit, bits)
    both = jnp.concatenate([x, swap(x, bit, bits), x], axis=-1)
    return cols(both, h * w, 2 * w)


def on_device(templates, leaf_inverse, v_basis, u_basis, coupling):
    bits = bit_axes()
    levels, pixels, rank = v_basis.shape
    width = templates.shape[1]
    c0 = jnp.dot(leaf_inverse, templates, preferred_element_type=F32)

    cross = jnp.einsum("kis,lir->klrs", u_basis, v_basis, preferred_element_type=F32)
    counts = [levels - 1 - k for k in range(levels - 1)]
    suffix = jnp.concatenate(
        [cross[k, k + 1 :].reshape(-1, rank) for k in range(levels - 1)], axis=0
    )
    first_prep = suffix
    w_own, w_sib = [None] * levels, [None] * levels
    for b in range(levels - 1):
        n = counts[b] * rank
        got = swap(suffix, b, bits)
        w_own[b] = suffix[:n].reshape(counts[b], rank, rank)
        w_sib[b] = got[:n].reshape(counts[b], rank, rank)
        suffix = suffix[n:] + got[n:]
    couple_sib = [swap(coupling[s, 0], s, bits) for s in range(levels - 1)]

    vl = jnp.einsum("lir,ij->lrj", v_basis, leaf_inverse, preferred_element_type=F32)
    vl_hi = vl.astype(BF16)
    vl_lo = (vl - vl_hi.astype(F32)).astype(BF16)

    def project(lv, x):
        return jnp.einsum(
            "lrj,jt->lrt", vl_hi[lv], x, preferred_element_type=F32
        ) + jnp.einsum("lrj,jt->lrt", vl_lo[lv], x, preferred_element_type=F32)

    proj0 = project(slice(0, 1), templates)[0].astype(BF16)
    rest = None
    half = width // 2
    if levels > 1:
        h = side(0, bits)
        keep = project(slice(1, levels), cols(templates, h * half, half))
        send = project(slice(1, levels), cols(templates, (1 - h) * half, half))
        payload0 = jnp.concatenate(
            [proj0[:, :half], proj0[:, half:],
             send.astype(BF16).reshape((levels - 1) * rank, half)],
            axis=0,
        )
        payload0, first_prep = lax.optimization_barrier((payload0, first_prep))
        got0 = swap(payload0, 0, bits)
        theirs0 = jnp.concatenate([got0[:rank], got0[rank : 2 * rank]], axis=1)
        rest = keep + got0[2 * rank :].reshape(levels - 1, rank, half).astype(F32)
    else:
        theirs0 = swap(proj0, 0, bits)
    own_coefs = []
    for s in range(levels):
        if s == 0:
            mine_b, theirs_b = proj0, theirs0
        else:
            mine_b = rest[0].astype(BF16)
            rest = rest[1:]
            n = rest.shape[0]
            w = mine_b.shape[1] // 2
            parts = [mine_b[:, :w], mine_b[:, w:]]
            summed = n == 1 and s == levels - 2
            if summed:
                last = rest[0].astype(BF16)
                parts += [last[:, :w], last[:, w:]]
            elif n > 0:
                h = side(s, bits)
                keep = cols(rest, h * w, w)
                send = cols(rest, (1 - h) * w, w)
                parts.append(send.astype(BF16).reshape(n * rank, w))
            payload = jnp.concatenate(parts, axis=0)
            if s < levels - 1:
                payload, w_sib[s] = lax.optimization_barrier((payload, w_sib[s]))
            got = swap(payload, s, bits)
            theirs_b = jnp.concatenate([got[:rank], got[rank : 2 * rank]], axis=1)
            if summed:
                recv = jnp.concatenate([got[2 * rank : 3 * rank], got[3 * rank :]], axis=1)
                rest = rest + recv.astype(F32)[None]
            elif n > 0:
                recv = got[2 * rank :].reshape(n, rank, w).astype(F32)
                rest = keep + recv
        lower = side(s, bits) == 0
        stacked = jnp.where(
            lower,
            jnp.concatenate([mine_b, theirs_b], axis=0),
            jnp.concatenate([theirs_b, mine_b], axis=0),
        )
        if s == 0:
            stacked, couple_sib = lax.optimization_barrier((stacked, couple_sib))
        coefs = jnp.dot(coupling[s, 0], stacked, preferred_element_type=F32).astype(BF16)
        own_coefs.append(coefs)
        if s < levels - 1:
            sib = jnp.dot(couple_sib[s], stacked, preferred_element_type=F32).astype(BF16)
            w = coefs.shape[1] // 2
            if rest.shape[-1] == coefs.shape[1]:
                co, cs = coefs, sib
            else:
                h = side(s, bits)
                co, cs = cols(coefs, h * w, w), cols(sib, h * w, w)
            fix = jnp.einsum(
                "nrs,st->nrt", w_own[s], co.astype(F32),
                preferred_element_type=F32, precision=lax.Precision.HIGHEST,
            ) + jnp.einsum(
                "nrs,st->nrt", w_sib[s], cs.astype(F32),
                preferred_element_type=F32, precision=lax.Precision.HIGHEST,
            )
            rest = rest - fix.reshape(rest.shape)

    full = [own_coefs[0]] + [None] * (levels - 1)
    pending = {s: own_coefs[s] for s in range(1, levels)}
    top = {s: s - 1 for s in range(1, levels)}
    if levels > 2:
        top[levels - 1] = levels - 3
    for j in reversed(range(levels - 1)):
        group = [s for s in range(1, levels) if top[s] >= j]
        if not group:
            continue
        joined = gather_half(jnp.stack([pending[s] for s in group]), j, bits)
        for i, s in enumerate(group):
            pending[s] = joined[i]
    for s in range(1, levels):
        full[s] = pending[s]
    current = c0
    for s in range(levels):
        current = current - jnp.dot(u_basis[s], full[s], preferred_element_type=F32)
    return current.astype(BF16)


def solution(mesh):
    placed = (
        P(("slab", "wide", "narrow", "inner"), None),
        P(("slab", "wide", "narrow", "inner"), None),
        P(None, ("slab", "wide", "narrow", "inner"), None),
        P(None, ("slab", "wide", "narrow", "inner"), None),
        P(None, ("slab", "wide", "narrow", "inner"), None, None),
    )
    return jax.shard_map(
        on_device,
        mesh=mesh,
        in_specs=placed,
        out_specs=P(("slab", "wide", "narrow", "inner"), None),
        check_vma=False,
    )
```

```python
import jax
import jax.numpy as jnp
from jax import lax
from jax.sharding import PartitionSpec as P

F32 = jnp.float32
BF16 = jnp.bfloat16


def bit_axes():
    bits = []
    for axis in ("inner", "narrow", "wide"):
        for stride in range(lax.axis_size(axis).bit_length() - 1):
            bits.append((axis, stride))
    return bits


def swap(x, bit, bits):
    axis, stride = bits[bit]
    n = lax.axis_size(axis)
    return lax.ppermute(x, axis, [(i, i ^ (1 << stride)) for i in range(n)])


def side(bit, bits):
    axis, stride = bits[bit]
    return (lax.axis_index(axis) >> stride) & 1


def cols(x, start, width):
    return lax.dynamic_slice_in_dim(x, start, width, axis=x.ndim - 1)


def reduce_half(x, bit, bits):
    w = x.shape[-1] // 2
    h = side(bit, bits)
    keep = cols(x, h * w, w)
    send = cols(x, (1 - h) * w, w)
    return keep + swap(send, bit, bits)


def gather_half(x, bit, bits):
    w = x.shape[-1]
    h = side(bit, bits)
    both = jnp.concatenate([x, swap(x, bit, bits), x], axis=-1)
    return cols(both, h * w, 2 * w)


def on_device(templates, leaf_inverse, v_basis, u_basis, coupling):
    bits = bit_axes()
    levels, pixels, rank = v_basis.shape
    width = templates.shape[1]
    c0 = jnp.dot(leaf_inverse, templates, preferred_element_type=F32)

    mine_c = coupling[:, 0]
    partial = [
        jnp.einsum(
            "lir,is->lrs", v_basis[s + 1:], u_basis[s], preferred_element_type=F32
        ).reshape(-1, rank)
        for s in range(levels - 1)
    ]
    w_own, theirs_c = [None] * levels, []
    for b in range(levels):
        c = mine_c[b]
        parts = [jnp.concatenate([c[:, :rank], c[:, rank:]], axis=0).astype(F32)]
        parts += partial[b:]
        got = swap(jnp.concatenate(parts, axis=0), b, bits)
        theirs = got[: 2 * rank].astype(BF16)
        theirs_c.append(jnp.concatenate([theirs[:rank], theirs[rank:]], axis=1))
        at = 2 * rank
        for s in range(b, levels - 1):
            n = partial[s].shape[0]
            recv = got[at : at + n]
            at += n
            if s == b:
                w_own[s] = jnp.concatenate([partial[s], recv], axis=1)
            else:
                partial[s] = partial[s] + recv
    couple = []
    for s in range(levels):
        lower = side(s, bits) == 0
        mine, theirs = mine_c[s], theirs_c[s]
        first = jnp.concatenate([mine[:, :rank], theirs[:, :rank]], axis=0)
        second = jnp.concatenate([mine[:, rank:], theirs[:, rank:]], axis=0)
        couple.append(
            jnp.concatenate(
                [jnp.where(lower, first, second), jnp.where(lower, second, first)],
                axis=1,
            )
        )

    vl = jnp.einsum("lir,ij->lrj", v_basis, leaf_inverse, preferred_element_type=F32)
    vl_hi = vl.astype(BF16)
    vl_lo = (vl - vl_hi.astype(F32)).astype(BF16)

    def project(lv, x):
        return jnp.einsum(
            "lrj,jt->lrt", vl_hi[lv], x, preferred_element_type=F32
        ) + jnp.einsum("lrj,jt->lrt", vl_lo[lv], x, preferred_element_type=F32)

    proj0 = project(slice(0, 1), templates)[0]
    rest = None
    if levels > 1:
        half = width // 2
        h = side(0, bits)
        keep = project(slice(1, levels), cols(templates, h * half, half))
        send = project(slice(1, levels), cols(templates, (1 - h) * half, half))
        rest = keep + swap(send, 0, bits)
    own_coefs = []
    for s in range(levels):
        if s == 0:
            mine_b = proj0.astype(BF16)
            theirs_b = swap(mine_b, s, bits)
        else:
            mine_b = rest[0].astype(BF16)
            rest = rest[1:]
            n = rest.shape[0]
            w = mine_b.shape[1] // 2
            parts = [mine_b[:, :w], mine_b[:, w:]]
            summed = n == 1 and s == levels - 2
            if summed:
                last = rest[0].astype(BF16)
                parts += [last[:, :w], last[:, w:]]
            elif n > 0:
                h = side(s, bits)
                keep = cols(rest, h * w, w)
                send = cols(rest, (1 - h) * w, w)
                parts.append(send.astype(BF16).reshape(n * rank, w))
            got = swap(jnp.concatenate(parts, axis=0), s, bits)
            theirs_b = jnp.concatenate([got[:rank], got[rank : 2 * rank]], axis=1)
            if summed:
                recv = jnp.concatenate([got[2 * rank : 3 * rank], got[3 * rank :]], axis=1)
                rest = rest + recv.astype(F32)[None]
            elif n > 0:
                recv = got[2 * rank :].reshape(n, rank, w).astype(F32)
                rest = keep + recv
        stacked = jnp.concatenate([mine_b, theirs_b], axis=0)
        coefs = jnp.dot(couple[s], stacked, preferred_element_type=F32).astype(BF16)
        own_coefs.append(coefs[:rank])
        if s < levels - 1:
            w = coefs.shape[1] // 2
            if rest.shape[-1] == coefs.shape[1]:
                piece = coefs.astype(F32)
            else:
                piece = cols(coefs, side(s, bits) * w, w).astype(F32)
            fix = jnp.dot(
                w_own[s], piece, preferred_element_type=F32,
                precision=lax.Precision.HIGHEST,
            )
            rest = rest - fix.reshape(rest.shape)

    full = [own_coefs[0]] + [None] * (levels - 1)
    pending = {s: own_coefs[s] for s in range(1, levels)}
    top = {s: s - 1 for s in range(1, levels)}
    if levels > 2:
        top[levels - 1] = levels - 3
    early = c0 - jnp.dot(u_basis[0], own_coefs[0], preferred_element_type=F32)
    u_rest = jnp.transpose(u_basis[1:], (1, 0, 2)).reshape(pixels, (levels - 1) * rank)
    joined = None
    for j in reversed(range(levels - 1)):
        group = [s for s in range(1, levels) if top[s] >= j]
        if not group:
            continue
        joined = gather_half(jnp.stack([pending[s] for s in group]), j, bits)
        for i, s in enumerate(group):
            pending[s] = joined[i]
    if joined is None:
        joined = jnp.stack([pending[s] for s in range(1, levels)])
    current = early - jnp.dot(
        u_rest, joined.reshape((levels - 1) * rank, width), preferred_element_type=F32
    )
    return current.astype(BF16)


def solution(mesh):
    placed = (
        P(("slab", "wide", "narrow", "inner"), None),
        P(("slab", "wide", "narrow", "inner"), None),
        P(None, ("slab", "wide", "narrow", "inner"), None),
        P(None, ("slab", "wide", "narrow", "inner"), None),
        P(None, ("slab", "wide", "narrow", "inner"), None, None),
    )
    return jax.shard_map(
        on_device,
        mesh=mesh,
        in_specs=placed,
        out_specs=P(("slab", "wide", "narrow", "inner"), None),
        check_vma=False,
    )
```

```python
import jax
import jax.numpy as jnp
from jax import lax
from jax.sharding import PartitionSpec as P

F32 = jnp.float32
BF16 = jnp.bfloat16


def bit_axes():
    bits = []
    for axis in ("inner", "narrow", "wide"):
        for stride in range(lax.axis_size(axis).bit_length() - 1):
            bits.append((axis, stride))
    return bits


def swap(x, bit, bits):
    axis, stride = bits[bit]
    n = lax.axis_size(axis)
    return lax.ppermute(x, axis, [(i, i ^ (1 << stride)) for i in range(n)])


def side(bit, bits):
    axis, stride = bits[bit]
    return (lax.axis_index(axis) >> stride) & 1


def cols(x, start, width):
    return lax.dynamic_slice_in_dim(x, start, width, axis=x.ndim - 1)


def reduce_half(x, bit, bits):
    w = x.shape[-1] // 2
    h = side(bit, bits)
    keep = cols(x, h * w, w)
    send = cols(x, (1 - h) * w, w)
    return keep + swap(send, bit, bits)


def gather_half(x, bit, bits):
    w = x.shape[-1]
    h = side(bit, bits)
    both = jnp.concatenate([x, swap(x, bit, bits), x], axis=-1)
    return cols(both, h * w, 2 * w)


def on_device(templates, leaf_inverse, v_basis, u_basis, coupling):
    bits = bit_axes()
    levels, pixels, rank = v_basis.shape
    width = templates.shape[1]
    c0 = jnp.dot(leaf_inverse, templates, preferred_element_type=F32)

    mine_c = coupling[:, 0]
    partial = [
        jnp.einsum(
            "lir,is->lrs", v_basis[s + 1:], u_basis[s], preferred_element_type=F32
        ).reshape(-1, rank)
        for s in range(levels - 1)
    ]
    w_own = [None] * levels
    for b in range(levels - 1):
        got = swap(jnp.concatenate(partial[b:], axis=0), b, bits)
        at = 0
        for s in range(b, levels - 1):
            n = partial[s].shape[0]
            recv = got[at : at + n]
            at += n
            if s == b:
                w_own[s] = jnp.concatenate([partial[s], recv], axis=1)
            else:
                partial[s] = partial[s] + recv
    theirs_c = [swap(mine_c[s], s, bits) for s in range(levels)]

    def ordered(s, theirs):
        lower = side(s, bits) == 0
        mine = mine_c[s]
        first = jnp.concatenate([mine[:, :rank], theirs[:, :rank]], axis=0)
        second = jnp.concatenate([mine[:, rank:], theirs[:, rank:]], axis=0)
        return jnp.concatenate(
            [jnp.where(lower, first, second), jnp.where(lower, second, first)],
            axis=1,
        )

    vl = jnp.einsum("lir,ij->lrj", v_basis, leaf_inverse, preferred_element_type=F32)
    vl_hi = vl.astype(BF16)
    vl_lo = (vl - vl_hi.astype(F32)).astype(BF16)

    def project(lv, x):
        return jnp.einsum(
            "lrj,jt->lrt", vl_hi[lv], x, preferred_element_type=F32
        ) + jnp.einsum("lrj,jt->lrt", vl_lo[lv], x, preferred_element_type=F32)

    proj0 = project(slice(0, 1), templates)[0]
    rest = None
    if levels > 1:
        half = width // 2
        h = side(0, bits)
        keep = project(slice(1, levels), cols(templates, h * half, half))
        send = project(slice(1, levels), cols(templates, (1 - h) * half, half))
        rest = keep + swap(send, 0, bits)
    own_coefs = []
    for s in range(levels):
        if s == 0:
            mine_b = proj0.astype(BF16)
            theirs_b = swap(mine_b, s, bits)
        else:
            mine_b = rest[0].astype(BF16)
            rest = rest[1:]
            n = rest.shape[0]
            w = mine_b.shape[1] // 2
            parts = [mine_b[:, :w], mine_b[:, w:]]
            summed = n == 1 and s == levels - 2
            if summed:
                last = rest[0].astype(BF16)
                parts += [last[:, :w], last[:, w:]]
            elif n > 0:
                h = side(s, bits)
                keep = cols(rest, h * w, w)
                send = cols(rest, (1 - h) * w, w)
                parts.append(send.astype(BF16).reshape(n * rank, w))
            got = swap(jnp.concatenate(parts, axis=0), s, bits)
            theirs_b = jnp.concatenate([got[:rank], got[rank : 2 * rank]], axis=1)
            if summed:
                recv = jnp.concatenate([got[2 * rank : 3 * rank], got[3 * rank :]], axis=1)
                rest = rest + recv.astype(F32)[None]
            elif n > 0:
                recv = got[2 * rank :].reshape(n, rank, w).astype(F32)
                rest = keep + recv
        stacked = jnp.concatenate([mine_b, theirs_b], axis=0)
        if s == 0:
            stacked, theirs_c = lax.optimization_barrier((stacked, theirs_c))
        couple = ordered(s, theirs_c[s])
        coefs = jnp.dot(couple, stacked, preferred_element_type=F32).astype(BF16)
        own_coefs.append(coefs[:rank])
        if s < levels - 1:
            w = coefs.shape[1] // 2
            if rest.shape[-1] == coefs.shape[1]:
                piece = coefs.astype(F32)
            else:
                piece = cols(coefs, side(s, bits) * w, w).astype(F32)
            fix = jnp.dot(
                w_own[s], piece, preferred_element_type=F32,
                precision=lax.Precision.HIGHEST,
            )
            rest = rest - fix.reshape(rest.shape)

    full = [own_coefs[0]] + [None] * (levels - 1)
    pending = {s: own_coefs[s] for s in range(1, levels)}
    top = {s: s - 1 for s in range(1, levels)}
    if levels > 2:
        top[levels - 1] = levels - 3
    for j in reversed(range(levels - 1)):
        group = [s for s in range(1, levels) if top[s] >= j]
        if not group:
            continue
        joined = gather_half(jnp.stack([pending[s] for s in group]), j, bits)
        for i, s in enumerate(group):
            pending[s] = joined[i]
    for s in range(1, levels):
        full[s] = pending[s]
    current = c0
    for s in range(levels):
        current = current - jnp.dot(u_basis[s], full[s], preferred_element_type=F32)
    return current.astype(BF16)


def solution(mesh):
    placed = (
        P(("slab", "wide", "narrow", "inner"), None),
        P(("slab", "wide", "narrow", "inner"), None),
        P(None, ("slab", "wide", "narrow", "inner"), None),
        P(None, ("slab", "wide", "narrow", "inner"), None),
        P(None, ("slab", "wide", "narrow", "inner"), None, None),
    )
    return jax.shard_map(
        on_device,
        mesh=mesh,
        in_specs=placed,
        out_specs=P(("slab", "wide", "narrow", "inner"), None),
        check_vma=False,
    )
```

```python
import jax
import jax.numpy as jnp
from jax import lax
from jax.sharding import PartitionSpec as P

F32 = jnp.float32
BF16 = jnp.bfloat16


def bit_axes():
    bits = []
    for axis in ("inner", "narrow", "wide"):
        for stride in range(lax.axis_size(axis).bit_length() - 1):
            bits.append((axis, stride))
    return bits


def swap(x, bit, bits):
    axis, stride = bits[bit]
    n = lax.axis_size(axis)
    return lax.ppermute(x, axis, [(i, i ^ (1 << stride)) for i in range(n)])


def side(bit, bits):
    axis, stride = bits[bit]
    return (lax.axis_index(axis) >> stride) & 1


def cols(x, start, width):
    return lax.dynamic_slice_in_dim(x, start, width, axis=x.ndim - 1)


def reduce_half(x, bit, bits):
    w = x.shape[-1] // 2
    h = side(bit, bits)
    keep = cols(x, h * w, w)
    send = cols(x, (1 - h) * w, w)
    return keep + swap(send, bit, bits)


def gather_half(x, bit, bits):
    w = x.shape[-1]
    h = side(bit, bits)
    both = jnp.concatenate([x, swap(x, bit, bits), x], axis=-1)
    return cols(both, h * w, 2 * w)


def on_device(templates, leaf_inverse, v_basis, u_basis, coupling):
    bits = bit_axes()
    levels, pixels, rank = v_basis.shape
    width = templates.shape[1]
    c0 = jnp.dot(leaf_inverse, templates, preferred_element_type=F32)

    mine_c = coupling[:, 0]
    partial = [
        jnp.einsum(
            "lir,is->lrs", v_basis[s + 1:], u_basis[s], preferred_element_type=F32
        ).reshape(-1, rank)
        for s in range(levels - 1)
    ]
    w_own, theirs_c = [None] * levels, []
    for b in range(levels):
        c = mine_c[b]
        parts = [jnp.concatenate([c[:, :rank], c[:, rank:]], axis=0).astype(F32)]
        parts += partial[b:]
        got = swap(jnp.concatenate(parts, axis=0), b, bits)
        theirs = got[: 2 * rank].astype(BF16)
        theirs_c.append(jnp.concatenate([theirs[:rank], theirs[rank:]], axis=1))
        at = 2 * rank
        for s in range(b, levels - 1):
            n = partial[s].shape[0]
            recv = got[at : at + n]
            at += n
            if s == b:
                w_own[s] = jnp.concatenate([partial[s], recv], axis=1)
            else:
                partial[s] = partial[s] + recv
    couple = []
    for s in range(levels):
        lower = side(s, bits) == 0
        mine, theirs = mine_c[s], theirs_c[s]
        first = jnp.concatenate([mine[:, :rank], theirs[:, :rank]], axis=0)
        second = jnp.concatenate([mine[:, rank:], theirs[:, rank:]], axis=0)
        couple.append(
            jnp.concatenate(
                [jnp.where(lower, first, second), jnp.where(lower, second, first)],
                axis=1,
            )
        )

    vl = jnp.einsum("lir,ij->lrj", v_basis, leaf_inverse, preferred_element_type=F32)
    vl_hi = vl.astype(BF16)
    vl_lo = (vl - vl_hi.astype(F32)).astype(BF16)

    def project(lv, x):
        return jnp.einsum(
            "lrj,jt->lrt", vl_hi[lv], x, preferred_element_type=F32
        ) + jnp.einsum("lrj,jt->lrt", vl_lo[lv], x, preferred_element_type=F32)

    proj0 = project(slice(0, 1), templates)[0]
    rest = None
    if levels > 1:
        half = width // 2
        h = side(0, bits)
        keep = project(slice(1, levels), cols(templates, h * half, half))
        send = project(slice(1, levels), cols(templates, (1 - h) * half, half))
        rest = keep + swap(send, 0, bits)
    own_coefs = []
    for s in range(levels):
        if s == 0:
            mine_b = proj0.astype(BF16)
            theirs_b = swap(mine_b, s, bits)
        else:
            mine_b = rest[0].astype(BF16)
            rest = rest[1:]
            n = rest.shape[0]
            w = mine_b.shape[1] // 2
            parts = [mine_b[:, :w], mine_b[:, w:]]
            summed = n == 1 and s == levels - 2
            if summed:
                last = rest[0].astype(BF16)
                parts += [last[:, :w], last[:, w:]]
            elif n > 0:
                h = side(s, bits)
                keep = cols(rest, h * w, w)
                send = cols(rest, (1 - h) * w, w)
                parts.append(send.astype(BF16).reshape(n * rank, w))
            got = swap(jnp.concatenate(parts, axis=0), s, bits)
            if s == levels - 1:
                early = c0 - jnp.dot(
                    u_basis[0], own_coefs[0], preferred_element_type=F32
                )
                got, early = lax.optimization_barrier((got, early))
            theirs_b = jnp.concatenate([got[:rank], got[rank : 2 * rank]], axis=1)
            if summed:
                recv = jnp.concatenate([got[2 * rank : 3 * rank], got[3 * rank :]], axis=1)
                rest = rest + recv.astype(F32)[None]
            elif n > 0:
                recv = got[2 * rank :].reshape(n, rank, w).astype(F32)
                rest = keep + recv
        stacked = jnp.concatenate([mine_b, theirs_b], axis=0)
        coefs = jnp.dot(couple[s], stacked, preferred_element_type=F32).astype(BF16)
        own_coefs.append(coefs[:rank])
        if s < levels - 1:
            w = coefs.shape[1] // 2
            if rest.shape[-1] == coefs.shape[1]:
                piece = coefs.astype(F32)
            else:
                piece = cols(coefs, side(s, bits) * w, w).astype(F32)
            fix = jnp.dot(
                w_own[s], piece, preferred_element_type=F32,
                precision=lax.Precision.HIGHEST,
            )
            rest = rest - fix.reshape(rest.shape)

    full = [own_coefs[0]] + [None] * (levels - 1)
    pending = {s: own_coefs[s] for s in range(1, levels)}
    top = {s: s - 1 for s in range(1, levels)}
    if levels > 2:
        top[levels - 1] = levels - 3
    for j in reversed(range(levels - 1)):
        group = [s for s in range(1, levels) if top[s] >= j]
        if not group:
            continue
        joined = gather_half(jnp.stack([pending[s] for s in group]), j, bits)
        for i, s in enumerate(group):
            pending[s] = joined[i]
    for s in range(1, levels):
        full[s] = pending[s]
    current = early
    for s in range(1, levels):
        current = current - jnp.dot(u_basis[s], full[s], preferred_element_type=F32)
    return current.astype(BF16)


def solution(mesh):
    placed = (
        P(("slab", "wide", "narrow", "inner"), None),
        P(("slab", "wide", "narrow", "inner"), None),
        P(None, ("slab", "wide", "narrow", "inner"), None),
        P(None, ("slab", "wide", "narrow", "inner"), None),
        P(None, ("slab", "wide", "narrow", "inner"), None, None),
    )
    return jax.shard_map(
        on_device,
        mesh=mesh,
        in_specs=placed,
        out_specs=P(("slab", "wide", "narrow", "inner"), None),
        check_vma=False,
    )
```

```python
import jax
import jax.numpy as jnp
from jax import lax
from jax.sharding import PartitionSpec as P

F32 = jnp.float32
BF16 = jnp.bfloat16


def bit_axes():
    bits = []
    for axis in ("inner", "narrow", "wide"):
        for stride in range(lax.axis_size(axis).bit_length() - 1):
            bits.append((axis, stride))
    return bits


def swap(x, bit, bits):
    axis, stride = bits[bit]
    n = lax.axis_size(axis)
    return lax.ppermute(x, axis, [(i, i ^ (1 << stride)) for i in range(n)])


def side(bit, bits):
    axis, stride = bits[bit]
    return (lax.axis_index(axis) >> stride) & 1


def cols(x, start, width):
    return lax.dynamic_slice_in_dim(x, start, width, axis=x.ndim - 1)


def reduce_half(x, bit, bits):
    w = x.shape[-1] // 2
    h = side(bit, bits)
    keep = cols(x, h * w, w)
    send = cols(x, (1 - h) * w, w)
    return keep + swap(send, bit, bits)


def gather_half(x, bit, bits):
    w = x.shape[-1]
    h = side(bit, bits)
    both = jnp.concatenate([x, swap(x, bit, bits), x], axis=-1)
    return cols(both, h * w, 2 * w)


def on_device(templates, leaf_inverse, v_basis, u_basis, coupling):
    bits = bit_axes()
    levels, pixels, rank = v_basis.shape
    width = templates.shape[1]
    c0 = jnp.dot(leaf_inverse, templates, preferred_element_type=F32)

    mine_c = coupling[:, 0]
    partial = [
        jnp.einsum(
            "lir,is->lrs", v_basis[s + 1:], u_basis[s], preferred_element_type=F32
        ).reshape(-1, rank)
        for s in range(levels - 1)
    ]
    w_own, theirs_c = [None] * levels, []
    for b in range(levels):
        c = mine_c[b]
        parts = [jnp.concatenate([c[:, :rank], c[:, rank:]], axis=0).astype(F32)]
        parts += partial[b:]
        got = swap(jnp.concatenate(parts, axis=0), b, bits)
        theirs = got[: 2 * rank].astype(BF16)
        theirs_c.append(jnp.concatenate([theirs[:rank], theirs[rank:]], axis=1))
        at = 2 * rank
        for s in range(b, levels - 1):
            n = partial[s].shape[0]
            recv = got[at : at + n]
            at += n
            if s == b:
                w_own[s] = jnp.concatenate([partial[s], recv], axis=1)
            else:
                partial[s] = partial[s] + recv
    couple = []
    for s in range(levels):
        lower = side(s, bits) == 0
        mine, theirs = mine_c[s], theirs_c[s]
        first = jnp.concatenate([mine[:, :rank], theirs[:, :rank]], axis=0)
        second = jnp.concatenate([mine[:, rank:], theirs[:, rank:]], axis=0)
        couple.append(
            jnp.concatenate(
                [jnp.where(lower, first, second), jnp.where(lower, second, first)],
                axis=1,
            )
        )

    vl = jnp.einsum("lir,ij->lrj", v_basis, leaf_inverse, preferred_element_type=F32)
    vl_hi = vl.astype(BF16)
    vl_lo = (vl - vl_hi.astype(F32)).astype(BF16)

    def project(lv, x):
        return jnp.einsum(
            "lrj,jt->lrt", vl_hi[lv], x, preferred_element_type=F32
        ) + jnp.einsum("lrj,jt->lrt", vl_lo[lv], x, preferred_element_type=F32)

    proj0 = project(slice(0, 1), templates)[0]
    rest = None
    if levels > 1:
        half = width // 2
        h = side(0, bits)
        keep = project(slice(1, levels), cols(templates, h * half, half))
        send = project(slice(1, levels), cols(templates, (1 - h) * half, half))
        rest = keep + swap(send, 0, bits)
    own_coefs = []
    for s in range(levels):
        if s == 0:
            mine_b = proj0.astype(BF16)
            theirs_b = swap(mine_b, s, bits)
        else:
            mine_b = rest[0].astype(BF16)
            rest = rest[1:]
            n = rest.shape[0]
            w = mine_b.shape[1] // 2
            parts = [mine_b[:, :w], mine_b[:, w:]]
            summed = n == 1 and s == levels - 2
            if summed:
                last = rest[0].astype(BF16)
                parts += [last[:, :w], last[:, w:]]
            elif n > 0:
                h = side(s, bits)
                keep = cols(rest, h * w, w)
                send = cols(rest, (1 - h) * w, w)
                parts.append(send.astype(BF16).reshape(n * rank, w))
            payload = jnp.concatenate(parts, axis=0)
            if s == levels - 1:
                payload, lin, tin, first = lax.optimization_barrier(
                    (payload, leaf_inverse, templates, own_coefs[0])
                )
                early = jnp.dot(lin, tin, preferred_element_type=F32) - jnp.dot(
                    u_basis[0], first, preferred_element_type=F32
                )
            got = swap(payload, s, bits)
            if s == levels - 1:
                got, early = lax.optimization_barrier((got, early))
            theirs_b = jnp.concatenate([got[:rank], got[rank : 2 * rank]], axis=1)
            if summed:
                recv = jnp.concatenate([got[2 * rank : 3 * rank], got[3 * rank :]], axis=1)
                rest = rest + recv.astype(F32)[None]
            elif n > 0:
                recv = got[2 * rank :].reshape(n, rank, w).astype(F32)
                rest = keep + recv
        stacked = jnp.concatenate([mine_b, theirs_b], axis=0)
        coefs = jnp.dot(couple[s], stacked, preferred_element_type=F32).astype(BF16)
        own_coefs.append(coefs[:rank])
        if s < levels - 1:
            w = coefs.shape[1] // 2
            if rest.shape[-1] == coefs.shape[1]:
                piece = coefs.astype(F32)
            else:
                piece = cols(coefs, side(s, bits) * w, w).astype(F32)
            fix = jnp.dot(
                w_own[s], piece, preferred_element_type=F32,
                precision=lax.Precision.HIGHEST,
            )
            rest = rest - fix.reshape(rest.shape)

    full = [own_coefs[0]] + [None] * (levels - 1)
    pending = {s: own_coefs[s] for s in range(1, levels)}
    top = {s: s - 1 for s in range(1, levels)}
    if levels > 2:
        top[levels - 1] = levels - 3
    for j in reversed(range(levels - 1)):
        group = [s for s in range(1, levels) if top[s] >= j]
        if not group:
            continue
        joined = gather_half(jnp.stack([pending[s] for s in group]), j, bits)
        for i, s in enumerate(group):
            pending[s] = joined[i]
    for s in range(1, levels):
        full[s] = pending[s]
    current = early
    for s in range(1, levels):
        current = current - jnp.dot(u_basis[s], full[s], preferred_element_type=F32)
    return current.astype(BF16)


def solution(mesh):
    placed = (
        P(("slab", "wide", "narrow", "inner"), None),
        P(("slab", "wide", "narrow", "inner"), None),
        P(None, ("slab", "wide", "narrow", "inner"), None),
        P(None, ("slab", "wide", "narrow", "inner"), None),
        P(None, ("slab", "wide", "narrow", "inner"), None, None),
    )
    return jax.shard_map(
        on_device,
        mesh=mesh,
        in_specs=placed,
        out_specs=P(("slab", "wide", "narrow", "inner"), None),
        check_vma=False,
    )
```

```python
import jax
import jax.numpy as jnp
from jax import lax
from jax.sharding import PartitionSpec as P

F32 = jnp.float32
BF16 = jnp.bfloat16


def bit_axes():
    bits = []
    for axis in ("inner", "narrow", "wide"):
        for stride in range(lax.axis_size(axis).bit_length() - 1):
            bits.append((axis, stride))
    return bits


def swap(x, bit, bits):
    axis, stride = bits[bit]
    n = lax.axis_size(axis)
    return lax.ppermute(x, axis, [(i, i ^ (1 << stride)) for i in range(n)])


def side(bit, bits):
    axis, stride = bits[bit]
    return (lax.axis_index(axis) >> stride) & 1


def cols(x, start, width):
    return lax.dynamic_slice_in_dim(x, start, width, axis=x.ndim - 1)


def reduce_half(x, bit, bits):
    w = x.shape[-1] // 2
    h = side(bit, bits)
    keep = cols(x, h * w, w)
    send = cols(x, (1 - h) * w, w)
    return keep + swap(send, bit, bits)


def gather_half(x, bit, bits):
    w = x.shape[-1]
    h = side(bit, bits)
    both = jnp.concatenate([x, swap(x, bit, bits), x], axis=-1)
    return cols(both, h * w, 2 * w)


def on_device(templates, leaf_inverse, v_basis, u_basis, coupling):
    bits = bit_axes()
    levels, pixels, rank = v_basis.shape
    width = templates.shape[1]
    c0 = jnp.dot(leaf_inverse, templates, preferred_element_type=F32)

    mine_c = coupling[:, 0]
    partial = [
        jnp.einsum(
            "lir,is->lrs", v_basis[s + 1:], u_basis[s], preferred_element_type=F32
        ).reshape(-1, rank)
        for s in range(levels - 1)
    ]
    w_own, theirs_c = [None] * levels, []
    for b in range(levels):
        c = mine_c[b]
        parts = [jnp.concatenate([c[:, :rank], c[:, rank:]], axis=0).astype(F32)]
        parts += partial[b:]
        got = swap(jnp.concatenate(parts, axis=0), b, bits)
        theirs = got[: 2 * rank].astype(BF16)
        theirs_c.append(jnp.concatenate([theirs[:rank], theirs[rank:]], axis=1))
        at = 2 * rank
        for s in range(b, levels - 1):
            n = partial[s].shape[0]
            recv = got[at : at + n]
            at += n
            if s == b:
                w_own[s] = jnp.concatenate([partial[s], recv], axis=1)
            else:
                partial[s] = partial[s] + recv
    couple = []
    for s in range(levels):
        lower = side(s, bits) == 0
        mine, theirs = mine_c[s], theirs_c[s]
        first = jnp.concatenate([mine[:, :rank], theirs[:, :rank]], axis=0)
        second = jnp.concatenate([mine[:, rank:], theirs[:, rank:]], axis=0)
        couple.append(
            jnp.concatenate(
                [jnp.where(lower, first, second), jnp.where(lower, second, first)],
                axis=1,
            )
        )

    vl = jnp.einsum("lir,ij->lrj", v_basis, leaf_inverse, preferred_element_type=F32)
    vl_hi = vl.astype(BF16)
    vl_lo = (vl - vl_hi.astype(F32)).astype(BF16)

    def project(lv, x):
        return jnp.einsum(
            "lrj,jt->lrt", vl_hi[lv], x, preferred_element_type=F32
        ) + jnp.einsum("lrj,jt->lrt", vl_lo[lv], x, preferred_element_type=F32)

    proj0 = project(slice(0, 1), templates)[0]
    rest = None
    if levels > 1:
        half = width // 2
        h = side(0, bits)
        keep = project(slice(1, levels), cols(templates, h * half, half))
        send = project(slice(1, levels), cols(templates, (1 - h) * half, half))
        rest = keep + swap(send, 0, bits)
    own_coefs = []
    for s in range(levels):
        if s == 0:
            mine_b = proj0.astype(BF16)
            theirs_b = swap(mine_b, s, bits)
        else:
            mine_b = rest[0].astype(BF16)
            rest = rest[1:]
            n = rest.shape[0]
            w = mine_b.shape[1] // 2
            parts = [mine_b[:, :w], mine_b[:, w:]]
            summed = n == 1 and s == levels - 2
            if summed:
                last = rest[0].astype(BF16)
                parts += [last[:, :w], last[:, w:]]
            elif n > 0:
                h = side(s, bits)
                keep = cols(rest, h * w, w)
                send = cols(rest, (1 - h) * w, w)
                parts.append(send.astype(BF16).reshape(n * rank, w))
            got = swap(jnp.concatenate(parts, axis=0), s, bits)
            theirs_b = jnp.concatenate([got[:rank], got[rank : 2 * rank]], axis=1)
            if summed:
                recv = jnp.concatenate([got[2 * rank : 3 * rank], got[3 * rank :]], axis=1)
                rest = rest + recv.astype(F32)[None]
            elif n > 0:
                recv = got[2 * rank :].reshape(n, rank, w).astype(F32)
                rest = keep + recv
        stacked = jnp.concatenate([mine_b, theirs_b], axis=0)
        coefs = jnp.dot(couple[s], stacked, preferred_element_type=F32).astype(BF16)
        own_coefs.append(coefs[:rank])
        if s < levels - 1:
            w = coefs.shape[1] // 2
            if rest.shape[-1] == coefs.shape[1]:
                piece = coefs.astype(F32)
            else:
                piece = cols(coefs, side(s, bits) * w, w).astype(F32)
            fix = jnp.dot(
                w_own[s], piece, preferred_element_type=F32,
                precision=lax.Precision.HIGHEST,
            )
            rest = rest - fix.reshape(rest.shape)

    pending = {s: own_coefs[s] for s in range(1, levels)}
    top = {s: s - 1 for s in range(1, levels)}
    if levels > 2:
        top[levels - 1] = levels - 3
    for j in reversed(range(1, levels - 1)):
        group = [s for s in range(1, levels) if top[s] >= j]
        if not group:
            continue
        joined = gather_half(jnp.stack([pending[s] for s in group]), j, bits)
        for i, s in enumerate(group):
            pending[s] = joined[i]
    half = width // 2
    h = side(0, bits)
    base = c0 - jnp.dot(u_basis[0], own_coefs[0], preferred_element_type=F32)
    mine = jnp.stack([pending[s] for s in range(1, levels)])
    theirs = swap(mine, 0, bits)

    def part(pieces, start):
        acc = cols(base, start, half)
        for i, s in enumerate(range(1, levels)):
            acc = acc - jnp.dot(u_basis[s], pieces[i], preferred_element_type=F32)
        return acc

    p_mine = part(mine, h * half)
    p_theirs = part(theirs, (1 - h) * half)
    current = jnp.where(
        h == 0,
        jnp.concatenate([p_mine, p_theirs], axis=1),
        jnp.concatenate([p_theirs, p_mine], axis=1),
    )
    return current.astype(BF16)


def solution(mesh):
    placed = (
        P(("slab", "wide", "narrow", "inner"), None),
        P(("slab", "wide", "narrow", "inner"), None),
        P(None, ("slab", "wide", "narrow", "inner"), None),
        P(None, ("slab", "wide", "narrow", "inner"), None),
        P(None, ("slab", "wide", "narrow", "inner"), None, None),
    )
    return jax.shard_map(
        on_device,
        mesh=mesh,
        in_specs=placed,
        out_specs=P(("slab", "wide", "narrow", "inner"), None),
        check_vma=False,
    )
```

```python
import jax
import jax.numpy as jnp
from jax import lax
from jax.sharding import PartitionSpec as P

F32 = jnp.float32
BF16 = jnp.bfloat16


def bit_axes():
    bits = []
    for axis in ("inner", "narrow", "wide"):
        for stride in range(lax.axis_size(axis).bit_length() - 1):
            bits.append((axis, stride))
    return bits


def swap(x, bit, bits):
    axis, stride = bits[bit]
    n = lax.axis_size(axis)
    return lax.ppermute(x, axis, [(i, i ^ (1 << stride)) for i in range(n)])


def side(bit, bits):
    axis, stride = bits[bit]
    return (lax.axis_index(axis) >> stride) & 1


def cols(x, start, width):
    return lax.dynamic_slice_in_dim(x, start, width, axis=x.ndim - 1)


def reduce_half(x, bit, bits):
    w = x.shape[-1] // 2
    h = side(bit, bits)
    keep = cols(x, h * w, w)
    send = cols(x, (1 - h) * w, w)
    return keep + swap(send, bit, bits)


def gather_half(x, bit, bits):
    w = x.shape[-1]
    h = side(bit, bits)
    both = jnp.concatenate([x, swap(x, bit, bits), x], axis=-1)
    return cols(both, h * w, 2 * w)


def on_device(templates, leaf_inverse, v_basis, u_basis, coupling):
    bits = bit_axes()
    levels, pixels, rank = v_basis.shape
    width = templates.shape[1]
    c0 = jnp.dot(leaf_inverse, templates, preferred_element_type=F32)

    mine_c = coupling[:, 0]
    partial = [
        jnp.einsum(
            "lir,is->lrs", v_basis[s + 1:], u_basis[s], preferred_element_type=F32
        ).reshape(-1, rank)
        for s in range(levels - 1)
    ]
    w_own, theirs_c = [None] * levels, []
    for b in range(levels):
        c = mine_c[b]
        parts = [jnp.concatenate([c[:, :rank], c[:, rank:]], axis=0).astype(F32)]
        parts += partial[b:]
        got = swap(jnp.concatenate(parts, axis=0), b, bits)
        theirs = got[: 2 * rank].astype(BF16)
        theirs_c.append(jnp.concatenate([theirs[:rank], theirs[rank:]], axis=1))
        at = 2 * rank
        for s in range(b, levels - 1):
            n = partial[s].shape[0]
            recv = got[at : at + n]
            at += n
            if s == b:
                w_own[s] = jnp.concatenate([partial[s], recv], axis=1)
            else:
                partial[s] = partial[s] + recv
    couple = []
    for s in range(levels):
        lower = side(s, bits) == 0
        mine, theirs = mine_c[s], theirs_c[s]
        first = jnp.concatenate([mine[:, :rank], theirs[:, :rank]], axis=0)
        second = jnp.concatenate([mine[:, rank:], theirs[:, rank:]], axis=0)
        couple.append(
            jnp.concatenate(
                [jnp.where(lower, first, second), jnp.where(lower, second, first)],
                axis=1,
            )
        )

    vl = jnp.einsum("lir,ij->lrj", v_basis, leaf_inverse, preferred_element_type=F32)
    vl_hi = vl.astype(BF16)
    vl_lo = (vl - vl_hi.astype(F32)).astype(BF16)

    def project(lv, x):
        return jnp.einsum(
            "lrj,jt->lrt", vl_hi[lv], x, preferred_element_type=F32
        ) + jnp.einsum("lrj,jt->lrt", vl_lo[lv], x, preferred_element_type=F32)

    proj0 = project(slice(0, 1), templates)[0]
    rest = None
    if levels > 1:
        half = width // 2
        h = side(0, bits)
        keep = project(slice(1, levels), cols(templates, h * half, half))
        send = project(slice(1, levels), cols(templates, (1 - h) * half, half))
        rest = keep + swap(send, 0, bits)
    own_coefs = []
    for s in range(levels):
        if s == 0:
            mine_b = proj0.astype(BF16)
            theirs_b = swap(mine_b, s, bits)
        else:
            mine_b = rest[0].astype(BF16)
            rest = rest[1:]
            n = rest.shape[0]
            w = mine_b.shape[1] // 2
            parts = [mine_b[:, :w], mine_b[:, w:]]
            summed = n > 0
            if summed:
                later = rest.astype(BF16)
                parts += [later[:, :, :w].reshape(n * rank, w),
                          later[:, :, w:].reshape(n * rank, w)]
            elif n > 0:
                h = side(s, bits)
                keep = cols(rest, h * w, w)
                send = cols(rest, (1 - h) * w, w)
                parts.append(send.astype(BF16).reshape(n * rank, w))
            got = swap(jnp.concatenate(parts, axis=0), s, bits)
            theirs_b = jnp.concatenate([got[:rank], got[rank : 2 * rank]], axis=1)
            if summed:
                lo = got[2 * rank : (2 + n) * rank].reshape(n, rank, w)
                hi = got[(2 + n) * rank :].reshape(n, rank, w)
                rest = rest + jnp.concatenate([lo, hi], axis=2).astype(F32)
            elif n > 0:
                recv = got[2 * rank :].reshape(n, rank, w).astype(F32)
                rest = keep + recv
        stacked = jnp.concatenate([mine_b, theirs_b], axis=0)
        coefs = jnp.dot(couple[s], stacked, preferred_element_type=F32).astype(BF16)
        own_coefs.append(coefs[:rank])
        if s < levels - 1:
            w = coefs.shape[1] // 2
            if rest.shape[-1] == coefs.shape[1]:
                piece = coefs.astype(F32)
            else:
                piece = cols(coefs, side(s, bits) * w, w).astype(F32)
            fix = jnp.dot(
                w_own[s], piece, preferred_element_type=F32,
                precision=lax.Precision.HIGHEST,
            )
            rest = rest - fix.reshape(rest.shape)

    full = [own_coefs[0]] + [None] * (levels - 1)
    pending = {s: own_coefs[s] for s in range(1, levels)}
    top = {s: 0 for s in range(1, levels)}
    for j in reversed(range(levels - 1)):
        group = [s for s in range(1, levels) if top[s] >= j]
        if not group:
            continue
        joined = gather_half(jnp.stack([pending[s] for s in group]), j, bits)
        for i, s in enumerate(group):
            pending[s] = joined[i]
    for s in range(1, levels):
        full[s] = pending[s]
    current = c0
    for s in range(levels):
        current = current - jnp.dot(u_basis[s], full[s], preferred_element_type=F32)
    return current.astype(BF16)


def solution(mesh):
    placed = (
        P(("slab", "wide", "narrow", "inner"), None),
        P(("slab", "wide", "narrow", "inner"), None),
        P(None, ("slab", "wide", "narrow", "inner"), None),
        P(None, ("slab", "wide", "narrow", "inner"), None),
        P(None, ("slab", "wide", "narrow", "inner"), None, None),
    )
    return jax.shard_map(
        on_device,
        mesh=mesh,
        in_specs=placed,
        out_specs=P(("slab", "wide", "narrow", "inner"), None),
        check_vma=False,
    )
```

```python
import jax
import jax.numpy as jnp
from jax import lax
from jax.sharding import PartitionSpec as P

F32 = jnp.float32
BF16 = jnp.bfloat16


def bit_axes():
    bits = []
    for axis in ("inner", "narrow", "wide"):
        for stride in range(lax.axis_size(axis).bit_length() - 1):
            bits.append((axis, stride))
    return bits


def swap(x, bit, bits):
    axis, stride = bits[bit]
    n = lax.axis_size(axis)
    return lax.ppermute(x, axis, [(i, i ^ (1 << stride)) for i in range(n)])


def side(bit, bits):
    axis, stride = bits[bit]
    return (lax.axis_index(axis) >> stride) & 1


def cols(x, start, width):
    return lax.dynamic_slice_in_dim(x, start, width, axis=x.ndim - 1)


def reduce_half(x, bit, bits):
    w = x.shape[-1] // 2
    h = side(bit, bits)
    keep = cols(x, h * w, w)
    send = cols(x, (1 - h) * w, w)
    return keep + swap(send, bit, bits)


def gather_half(x, bit, bits):
    w = x.shape[-1]
    h = side(bit, bits)
    both = jnp.concatenate([x, swap(x, bit, bits), x], axis=-1)
    return cols(both, h * w, 2 * w)


def on_device(templates, leaf_inverse, v_basis, u_basis, coupling):
    bits = bit_axes()
    levels, pixels, rank = v_basis.shape
    width = templates.shape[1]
    c0 = jnp.dot(leaf_inverse, templates, preferred_element_type=F32)

    mine_c = coupling[:, 0]
    partial = [
        jnp.einsum(
            "lir,is->lrs", v_basis[s + 1:], u_basis[s], preferred_element_type=F32
        ).reshape(-1, rank)
        for s in range(levels - 1)
    ]
    w_own, theirs_c = [None] * levels, []
    for b in range(levels):
        c = mine_c[b]
        parts = [jnp.concatenate([c[:, :rank], c[:, rank:]], axis=0).astype(F32)]
        parts += partial[b:]
        got = swap(jnp.concatenate(parts, axis=0), b, bits)
        theirs = got[: 2 * rank]
        theirs_c.append(jnp.concatenate([theirs[:rank], theirs[rank:]], axis=1))
        at = 2 * rank
        for s in range(b, levels - 1):
            n = partial[s].shape[0]
            recv = got[at : at + n]
            at += n
            if s == b:
                w_own[s] = jnp.concatenate([partial[s], recv], axis=1)
            else:
                partial[s] = partial[s] + recv
    couple = []
    for s in range(levels):
        lower = side(s, bits) == 0
        mine, theirs = mine_c[s], theirs_c[s]
        first = jnp.concatenate([mine[:, :rank], theirs[:, :rank]], axis=0)
        second = jnp.concatenate([mine[:, rank:], theirs[:, rank:]], axis=0)
        couple.append(
            jnp.concatenate(
                [jnp.where(lower, first, second), jnp.where(lower, second, first)],
                axis=1,
            )
        )

    vl = jnp.einsum("lir,ij->lrj", v_basis, leaf_inverse, preferred_element_type=F32)
    vl_hi = vl.astype(BF16)
    vl_lo = (vl - vl_hi.astype(F32)).astype(BF16)

    def project(lv, x):
        return jnp.einsum(
            "lrj,jt->lrt", vl_hi[lv], x, preferred_element_type=F32
        ) + jnp.einsum("lrj,jt->lrt", vl_lo[lv], x, preferred_element_type=F32)

    proj0 = project(slice(0, 1), templates)[0]
    rest = None
    if levels > 1:
        half = width // 2
        h = side(0, bits)
        keep = project(slice(1, levels), cols(templates, h * half, half))
        send = project(slice(1, levels), cols(templates, (1 - h) * half, half))
        rest = keep + swap(send, 0, bits)
    own_coefs = []
    for s in range(levels):
        if s == 0:
            mine_b = proj0.astype(BF16)
            theirs_b = swap(mine_b, s, bits)
        else:
            mine_b = rest[0].astype(BF16)
            rest = rest[1:]
            n = rest.shape[0]
            w = mine_b.shape[1] // 2
            parts = [mine_b[:, :w], mine_b[:, w:]]
            summed = n == 1 and s == levels - 2
            if summed:
                last = rest[0].astype(BF16)
                parts += [last[:, :w], last[:, w:]]
            elif n > 0:
                h = side(s, bits)
                keep = cols(rest, h * w, w)
                send = cols(rest, (1 - h) * w, w)
                parts.append(send.astype(BF16).reshape(n * rank, w))
            got = swap(jnp.concatenate(parts, axis=0), s, bits)
            theirs_b = jnp.concatenate([got[:rank], got[rank : 2 * rank]], axis=1)
            if summed:
                recv = jnp.concatenate([got[2 * rank : 3 * rank], got[3 * rank :]], axis=1)
                rest = rest + recv.astype(F32)[None]
            elif n > 0:
                recv = got[2 * rank :].reshape(n, rank, w).astype(F32)
                rest = keep + recv
        stacked = jnp.concatenate([mine_b, theirs_b], axis=0)
        coefs = jnp.dot(couple[s], stacked, preferred_element_type=F32).astype(BF16)
        own_coefs.append(coefs[:rank])
        if s < levels - 1:
            w = coefs.shape[1] // 2
            if rest.shape[-1] == coefs.shape[1]:
                piece = coefs.astype(F32)
            else:
                piece = cols(coefs, side(s, bits) * w, w).astype(F32)
            fix = jnp.dot(
                w_own[s], piece, preferred_element_type=F32,
                precision=lax.Precision.HIGHEST,
            )
            rest = rest - fix.reshape(rest.shape)

    full = [own_coefs[0]] + [None] * (levels - 1)
    pending = {s: own_coefs[s] for s in range(1, levels)}
    top = {s: s - 1 for s in range(1, levels)}
    if levels > 2:
        top[levels - 1] = levels - 3
    for j in reversed(range(levels - 1)):
        group = [s for s in range(1, levels) if top[s] >= j]
        if not group:
            continue
        joined = gather_half(jnp.stack([pending[s] for s in group]), j, bits)
        for i, s in enumerate(group):
            pending[s] = joined[i]
    for s in range(1, levels):
        full[s] = pending[s]
    current = c0
    for s in range(levels):
        current = current - jnp.dot(u_basis[s], full[s], preferred_element_type=F32)
    return current.astype(BF16)


def solution(mesh):
    placed = (
        P(("slab", "wide", "narrow", "inner"), None),
        P(("slab", "wide", "narrow", "inner"), None),
        P(None, ("slab", "wide", "narrow", "inner"), None),
        P(None, ("slab", "wide", "narrow", "inner"), None),
        P(None, ("slab", "wide", "narrow", "inner"), None, None),
    )
    return jax.shard_map(
        on_device,
        mesh=mesh,
        in_specs=placed,
        out_specs=P(("slab", "wide", "narrow", "inner"), None),
        check_vma=False,
    )
```

```python
import jax
import jax.numpy as jnp
from jax import lax
from jax.sharding import PartitionSpec as P

F32 = jnp.float32
BF16 = jnp.bfloat16


def bit_axes():
    bits = []
    for axis in ("inner", "narrow", "wide"):
        for stride in range(lax.axis_size(axis).bit_length() - 1):
            bits.append((axis, stride))
    return bits


def swap(x, bit, bits):
    axis, stride = bits[bit]
    n = lax.axis_size(axis)
    return lax.ppermute(x, axis, [(i, i ^ (1 << stride)) for i in range(n)])


def side(bit, bits):
    axis, stride = bits[bit]
    return (lax.axis_index(axis) >> stride) & 1


def cols(x, start, width):
    return lax.dynamic_slice_in_dim(x, start, width, axis=x.ndim - 1)


def reduce_half(x, bit, bits):
    w = x.shape[-1] // 2
    h = side(bit, bits)
    keep = cols(x, h * w, w)
    send = cols(x, (1 - h) * w, w)
    return keep + swap(send, bit, bits)


def gather_half(x, bit, bits):
    w = x.shape[-1]
    h = side(bit, bits)
    both = jnp.concatenate([x, swap(x, bit, bits), x], axis=-1)
    return cols(both, h * w, 2 * w)


def on_device(templates, leaf_inverse, v_basis, u_basis, coupling):
    bits = bit_axes()
    levels, pixels, rank = v_basis.shape
    width = templates.shape[1]
    c0 = jnp.dot(leaf_inverse, templates, preferred_element_type=F32)

    mine_c = coupling[:, 0]
    partial = [
        jnp.einsum(
            "lir,is->lrs", v_basis[s + 1:], u_basis[s], preferred_element_type=F32
        ).reshape(-1, rank)
        for s in range(levels - 1)
    ]
    w_own, theirs_c = [None] * levels, []
    for b in range(levels):
        c = mine_c[b]
        parts = [jnp.concatenate([c[:, :rank], c[:, rank:]], axis=0).astype(F32)]
        parts += partial[b:]
        got = swap(jnp.concatenate(parts, axis=0), b, bits)
        theirs = got[: 2 * rank]
        theirs_c.append(jnp.concatenate([theirs[:rank], theirs[rank:]], axis=1))
        at = 2 * rank
        for s in range(b, levels - 1):
            n = partial[s].shape[0]
            recv = got[at : at + n]
            at += n
            if s == b:
                w_own[s] = (partial[s], recv)
            else:
                partial[s] = partial[s] + recv
    couple = []
    for s in range(levels):
        lower = side(s, bits) == 0
        mine, theirs = mine_c[s], theirs_c[s]
        first = jnp.concatenate([mine[:, :rank], theirs[:, :rank]], axis=0)
        second = jnp.concatenate([mine[:, rank:], theirs[:, rank:]], axis=0)
        couple.append(
            jnp.concatenate(
                [jnp.where(lower, first, second), jnp.where(lower, second, first)],
                axis=1,
            )
        )

    vl = jnp.einsum("lir,ij->lrj", v_basis, leaf_inverse, preferred_element_type=F32)
    vl_hi = vl.astype(BF16)
    vl_lo = (vl - vl_hi.astype(F32)).astype(BF16)

    def project(lv, x):
        return jnp.einsum(
            "lrj,jt->lrt", vl_hi[lv], x, preferred_element_type=F32
        ) + jnp.einsum("lrj,jt->lrt", vl_lo[lv], x, preferred_element_type=F32)

    proj0 = project(slice(0, 1), templates)[0]
    rest = None
    if levels > 1:
        half = width // 2
        h = side(0, bits)
        keep = project(slice(1, levels), cols(templates, h * half, half))
        send = project(slice(1, levels), cols(templates, (1 - h) * half, half))
        rest = keep + swap(send, 0, bits)
    own_coefs = []
    for s in range(levels):
        if s == 0:
            mine_b = proj0.astype(BF16)
            theirs_b = swap(mine_b, s, bits)
        else:
            mine_b = rest[0].astype(BF16)
            rest = rest[1:]
            n = rest.shape[0]
            w = mine_b.shape[1] // 2
            parts = [mine_b[:, :w], mine_b[:, w:]]
            summed = n == 1 and s == levels - 2
            if summed:
                last = rest[0].astype(BF16)
                parts += [last[:, :w], last[:, w:]]
            elif n > 0:
                h = side(s, bits)
                keep = cols(rest, h * w, w)
                send = cols(rest, (1 - h) * w, w)
                parts.append(send.astype(BF16).reshape(n * rank, w))
            got = swap(jnp.concatenate(parts, axis=0), s, bits)
            theirs_b = jnp.concatenate([got[:rank], got[rank : 2 * rank]], axis=1)
            if summed:
                recv = jnp.concatenate([got[2 * rank : 3 * rank], got[3 * rank :]], axis=1)
                rest = rest + recv.astype(F32)[None]
            elif n > 0:
                recv = got[2 * rank :].reshape(n, rank, w).astype(F32)
                rest = keep + recv
        stacked = jnp.concatenate([mine_b, theirs_b], axis=0)
        coefs = jnp.dot(couple[s], stacked, preferred_element_type=F32).astype(BF16)
        own_coefs.append(coefs[:rank])
        if s < levels - 1:
            w = coefs.shape[1] // 2
            if rest.shape[-1] == coefs.shape[1]:
                piece = coefs.astype(F32)
            else:
                piece = cols(coefs, side(s, bits) * w, w).astype(F32)
            own_w, sib_w = w_own[s]
            fix = jnp.dot(
                own_w, piece[:rank], preferred_element_type=F32,
                precision=lax.Precision.HIGHEST,
            ) + jnp.dot(
                sib_w, piece[rank:], preferred_element_type=F32,
                precision=lax.Precision.HIGHEST,
            )
            rest = rest - fix.reshape(rest.shape)

    full = [own_coefs[0]] + [None] * (levels - 1)
    pending = {s: own_coefs[s] for s in range(1, levels)}
    top = {s: s - 1 for s in range(1, levels)}
    if levels > 2:
        top[levels - 1] = levels - 3
    for j in reversed(range(levels - 1)):
        group = [s for s in range(1, levels) if top[s] >= j]
        if not group:
            continue
        joined = gather_half(jnp.stack([pending[s] for s in group]), j, bits)
        for i, s in enumerate(group):
            pending[s] = joined[i]
    for s in range(1, levels):
        full[s] = pending[s]
    current = c0
    for s in range(levels):
        current = current - jnp.dot(u_basis[s], full[s], preferred_element_type=F32)
    return current.astype(BF16)


def solution(mesh):
    placed = (
        P(("slab", "wide", "narrow", "inner"), None),
        P(("slab", "wide", "narrow", "inner"), None),
        P(None, ("slab", "wide", "narrow", "inner"), None),
        P(None, ("slab", "wide", "narrow", "inner"), None),
        P(None, ("slab", "wide", "narrow", "inner"), None, None),
    )
    return jax.shard_map(
        on_device,
        mesh=mesh,
        in_specs=placed,
        out_specs=P(("slab", "wide", "narrow", "inner"), None),
        check_vma=False,
    )
```

```python
import jax
import jax.numpy as jnp
from jax import lax
from jax.sharding import PartitionSpec as P

F32 = jnp.float32
BF16 = jnp.bfloat16


def bit_axes():
    bits = []
    for axis in ("inner", "narrow", "wide"):
        for stride in range(lax.axis_size(axis).bit_length() - 1):
            bits.append((axis, stride))
    return bits


def swap(x, bit, bits):
    axis, stride = bits[bit]
    n = lax.axis_size(axis)
    return lax.ppermute(x, axis, [(i, i ^ (1 << stride)) for i in range(n)])


def side(bit, bits):
    axis, stride = bits[bit]
    return (lax.axis_index(axis) >> stride) & 1


def cols(x, start, width):
    return lax.dynamic_slice_in_dim(x, start, width, axis=x.ndim - 1)


def reduce_half(x, bit, bits):
    w = x.shape[-1] // 2
    h = side(bit, bits)
    keep = cols(x, h * w, w)
    send = cols(x, (1 - h) * w, w)
    return keep + swap(send, bit, bits)


def gather_half(x, bit, bits):
    w = x.shape[-1]
    h = side(bit, bits)
    both = jnp.concatenate([x, swap(x, bit, bits), x], axis=-1)
    return cols(both, h * w, 2 * w)


def on_device(templates, leaf_inverse, v_basis, u_basis, coupling):
    bits = bit_axes()
    levels, pixels, rank = v_basis.shape
    width = templates.shape[1]
    c0 = jnp.dot(leaf_inverse, templates, preferred_element_type=F32)

    mine_c = coupling[:, 0]
    partial = [
        jnp.einsum(
            "lir,is->lrs", v_basis[s + 1:], u_basis[s], preferred_element_type=F32
        ).reshape(-1, rank)
        for s in range(levels - 1)
    ]
    w_own, theirs_c = [None] * levels, []
    for b in range(levels):
        c = mine_c[b]
        parts = [jnp.concatenate([c[:, :rank], c[:, rank:]], axis=0).astype(F32)]
        parts += partial[b:]
        got = swap(jnp.concatenate(parts, axis=0), b, bits)
        theirs = got[: 2 * rank]
        theirs_c.append(jnp.concatenate([theirs[:rank], theirs[rank:]], axis=1))
        at = 2 * rank
        for s in range(b, levels - 1):
            n = partial[s].shape[0]
            recv = got[at : at + n]
            at += n
            if s == b:
                w_own[s] = jnp.concatenate([partial[s], recv], axis=1)
            else:
                partial[s] = partial[s] + recv
    couple = [
        jnp.concatenate([mine_c[s].astype(F32), theirs_c[s]], axis=0)
        for s in range(levels)
    ]

    vl = jnp.einsum("lir,ij->lrj", v_basis, leaf_inverse, preferred_element_type=F32)
    vl_hi = vl.astype(BF16)
    vl_lo = (vl - vl_hi.astype(F32)).astype(BF16)

    def project(lv, x):
        return jnp.einsum(
            "lrj,jt->lrt", vl_hi[lv], x, preferred_element_type=F32
        ) + jnp.einsum("lrj,jt->lrt", vl_lo[lv], x, preferred_element_type=F32)

    proj0 = project(slice(0, 1), templates)[0]
    rest = None
    if levels > 1:
        half = width // 2
        h = side(0, bits)
        keep = project(slice(1, levels), cols(templates, h * half, half))
        send = project(slice(1, levels), cols(templates, (1 - h) * half, half))
        rest = keep + swap(send, 0, bits)
    own_coefs = []
    for s in range(levels):
        if s == 0:
            mine_b = proj0.astype(BF16)
            theirs_b = swap(mine_b, s, bits)
        else:
            mine_b = rest[0].astype(BF16)
            rest = rest[1:]
            n = rest.shape[0]
            w = mine_b.shape[1] // 2
            parts = [mine_b[:, :w], mine_b[:, w:]]
            summed = n == 1 and s == levels - 2
            if summed:
                last = rest[0].astype(BF16)
                parts += [last[:, :w], last[:, w:]]
            elif n > 0:
                h = side(s, bits)
                keep = cols(rest, h * w, w)
                send = cols(rest, (1 - h) * w, w)
                parts.append(send.astype(BF16).reshape(n * rank, w))
            got = swap(jnp.concatenate(parts, axis=0), s, bits)
            theirs_b = jnp.concatenate([got[:rank], got[rank : 2 * rank]], axis=1)
            if summed:
                recv = jnp.concatenate([got[2 * rank : 3 * rank], got[3 * rank :]], axis=1)
                rest = rest + recv.astype(F32)[None]
            elif n > 0:
                recv = got[2 * rank :].reshape(n, rank, w).astype(F32)
                rest = keep + recv
        lower = side(s, bits) == 0
        stacked = jnp.where(
            lower,
            jnp.concatenate([mine_b, theirs_b], axis=0),
            jnp.concatenate([theirs_b, mine_b], axis=0),
        )
        coefs = jnp.dot(couple[s], stacked, preferred_element_type=F32).astype(BF16)
        own_coefs.append(coefs[:rank])
        if s < levels - 1:
            w = coefs.shape[1] // 2
            if rest.shape[-1] == coefs.shape[1]:
                piece = coefs.astype(F32)
            else:
                piece = cols(coefs, side(s, bits) * w, w).astype(F32)
            fix = jnp.dot(
                w_own[s], piece, preferred_element_type=F32,
                precision=lax.Precision.HIGHEST,
            )
            rest = rest - fix.reshape(rest.shape)

    full = [own_coefs[0]] + [None] * (levels - 1)
    pending = {s: own_coefs[s] for s in range(1, levels)}
    top = {s: s - 1 for s in range(1, levels)}
    if levels > 2:
        top[levels - 1] = levels - 3
    for j in reversed(range(levels - 1)):
        group = [s for s in range(1, levels) if top[s] >= j]
        if not group:
            continue
        joined = gather_half(jnp.stack([pending[s] for s in group]), j, bits)
        for i, s in enumerate(group):
            pending[s] = joined[i]
    for s in range(1, levels):
        full[s] = pending[s]
    current = c0
    for s in range(levels):
        current = current - jnp.dot(u_basis[s], full[s], preferred_element_type=F32)
    return current.astype(BF16)


def solution(mesh):
    placed = (
        P(("slab", "wide", "narrow", "inner"), None),
        P(("slab", "wide", "narrow", "inner"), None),
        P(None, ("slab", "wide", "narrow", "inner"), None),
        P(None, ("slab", "wide", "narrow", "inner"), None),
        P(None, ("slab", "wide", "narrow", "inner"), None, None),
    )
    return jax.shard_map(
        on_device,
        mesh=mesh,
        in_specs=placed,
        out_specs=P(("slab", "wide", "narrow", "inner"), None),
        check_vma=False,
    )
```

```python
import jax
import jax.numpy as jnp
from jax import lax
from jax.sharding import PartitionSpec as P

F32 = jnp.float32
BF16 = jnp.bfloat16


def bit_axes():
    bits = []
    for axis in ("inner", "narrow", "wide"):
        for stride in range(lax.axis_size(axis).bit_length() - 1):
            bits.append((axis, stride))
    return bits


def swap(x, bit, bits):
    axis, stride = bits[bit]
    n = lax.axis_size(axis)
    return lax.ppermute(x, axis, [(i, i ^ (1 << stride)) for i in range(n)])


def side(bit, bits):
    axis, stride = bits[bit]
    return (lax.axis_index(axis) >> stride) & 1


def cols(x, start, width):
    return lax.dynamic_slice_in_dim(x, start, width, axis=x.ndim - 1)


def reduce_half(x, bit, bits):
    w = x.shape[-1] // 2
    h = side(bit, bits)
    keep = cols(x, h * w, w)
    send = cols(x, (1 - h) * w, w)
    return keep + swap(send, bit, bits)


def gather_half(x, bit, bits):
    w = x.shape[-1]
    h = side(bit, bits)
    both = jnp.concatenate([x, swap(x, bit, bits), x], axis=-1)
    return cols(both, h * w, 2 * w)


def on_device(templates, leaf_inverse, v_basis, u_basis, coupling):
    bits = bit_axes()
    levels, pixels, rank = v_basis.shape
    width = templates.shape[1]
    c0 = jnp.dot(leaf_inverse, templates, preferred_element_type=F32)

    mine_c = coupling[:, 0]
    partial = [
        jnp.einsum(
            "lir,is->lrs", v_basis[s + 1:], u_basis[s], preferred_element_type=F32
        ).reshape(-1, rank)
        for s in range(levels - 1)
    ]
    w_own, theirs_c = [None] * levels, []
    for b in range(levels):
        c = mine_c[b]
        if b == levels - 1:
            theirs_c.append(swap(c, b, bits))
            continue
        parts = [jnp.concatenate([c[:, :rank], c[:, rank:]], axis=0).astype(F32)]
        parts += partial[b:]
        got = swap(jnp.concatenate(parts, axis=0), b, bits)
        theirs = got[: 2 * rank]
        theirs_c.append(jnp.concatenate([theirs[:rank], theirs[rank:]], axis=1))
        at = 2 * rank
        for s in range(b, levels - 1):
            n = partial[s].shape[0]
            recv = got[at : at + n]
            at += n
            if s == b:
                w_own[s] = jnp.concatenate([partial[s], recv], axis=1)
            else:
                partial[s] = partial[s] + recv
    couple = []
    for s in range(levels):
        lower = side(s, bits) == 0
        mine, theirs = mine_c[s], theirs_c[s]
        first = jnp.concatenate([mine[:, :rank], theirs[:, :rank]], axis=0)
        second = jnp.concatenate([mine[:, rank:], theirs[:, rank:]], axis=0)
        couple.append(
            jnp.concatenate(
                [jnp.where(lower, first, second), jnp.where(lower, second, first)],
                axis=1,
            )
        )

    vl = jnp.einsum("lir,ij->lrj", v_basis, leaf_inverse, preferred_element_type=F32)
    vl_hi = vl.astype(BF16)
    vl_lo = (vl - vl_hi.astype(F32)).astype(BF16)

    def project(lv, x):
        return jnp.einsum(
            "lrj,jt->lrt", vl_hi[lv], x, preferred_element_type=F32
        ) + jnp.einsum("lrj,jt->lrt", vl_lo[lv], x, preferred_element_type=F32)

    proj0 = project(slice(0, 1), templates)[0]
    rest = None
    if levels > 1:
        half = width // 2
        h = side(0, bits)
        keep = project(slice(1, levels), cols(templates, h * half, half))
        send = project(slice(1, levels), cols(templates, (1 - h) * half, half))
        rest = keep + swap(send, 0, bits)
    own_coefs = []
    for s in range(levels):
        if s == 0:
            mine_b = proj0.astype(BF16)
            theirs_b = swap(mine_b, s, bits)
        else:
            mine_b = rest[0].astype(BF16)
            rest = rest[1:]
            n = rest.shape[0]
            w = mine_b.shape[1] // 2
            parts = [mine_b[:, :w], mine_b[:, w:]]
            summed = n == 1 and s == levels - 2
            if summed:
                last = rest[0].astype(BF16)
                parts += [last[:, :w], last[:, w:]]
            elif n > 0:
                h = side(s, bits)
                keep = cols(rest, h * w, w)
                send = cols(rest, (1 - h) * w, w)
                parts.append(send.astype(BF16).reshape(n * rank, w))
            got = swap(jnp.concatenate(parts, axis=0), s, bits)
            theirs_b = jnp.concatenate([got[:rank], got[rank : 2 * rank]], axis=1)
            if summed:
                recv = jnp.concatenate([got[2 * rank : 3 * rank], got[3 * rank :]], axis=1)
                rest = rest + recv.astype(F32)[None]
            elif n > 0:
                recv = got[2 * rank :].reshape(n, rank, w).astype(F32)
                rest = keep + recv
        stacked = jnp.concatenate([mine_b, theirs_b], axis=0)
        coefs = jnp.dot(couple[s], stacked, preferred_element_type=F32).astype(BF16)
        own_coefs.append(coefs[:rank])
        if s < levels - 1:
            w = coefs.shape[1] // 2
            if rest.shape[-1] == coefs.shape[1]:
                piece = coefs.astype(F32)
            else:
                piece = cols(coefs, side(s, bits) * w, w).astype(F32)
            fix = jnp.dot(
                w_own[s], piece, preferred_element_type=F32,
                precision=lax.Precision.HIGHEST,
            )
            rest = rest - fix.reshape(rest.shape)

    full = [own_coefs[0]] + [None] * (levels - 1)
    pending = {s: own_coefs[s] for s in range(1, levels)}
    top = {s: s - 1 for s in range(1, levels)}
    if levels > 2:
        top[levels - 1] = levels - 3
    for j in reversed(range(levels - 1)):
        group = [s for s in range(1, levels) if top[s] >= j]
        if not group:
            continue
        joined = gather_half(jnp.stack([pending[s] for s in group]), j, bits)
        for i, s in enumerate(group):
            pending[s] = joined[i]
    for s in range(1, levels):
        full[s] = pending[s]
    current = c0
    for s in range(levels):
        current = current - jnp.dot(u_basis[s], full[s], preferred_element_type=F32)
    return current.astype(BF16)


def solution(mesh):
    placed = (
        P(("slab", "wide", "narrow", "inner"), None),
        P(("slab", "wide", "narrow", "inner"), None),
        P(None, ("slab", "wide", "narrow", "inner"), None),
        P(None, ("slab", "wide", "narrow", "inner"), None),
        P(None, ("slab", "wide", "narrow", "inner"), None, None),
    )
    return jax.shard_map(
        on_device,
        mesh=mesh,
        in_specs=placed,
        out_specs=P(("slab", "wide", "narrow", "inner"), None),
        check_vma=False,
    )
```

```python
import jax
import jax.numpy as jnp
from jax import lax
from jax.sharding import PartitionSpec as P

F32 = jnp.float32
BF16 = jnp.bfloat16


def bit_axes():
    bits = []
    for axis in ("inner", "narrow", "wide"):
        for stride in range(lax.axis_size(axis).bit_length() - 1):
            bits.append((axis, stride))
    return bits


def swap(x, bit, bits):
    axis, stride = bits[bit]
    n = lax.axis_size(axis)
    return lax.ppermute(x, axis, [(i, i ^ (1 << stride)) for i in range(n)])


def side(bit, bits):
    axis, stride = bits[bit]
    return (lax.axis_index(axis) >> stride) & 1


def cols(x, start, width):
    return lax.dynamic_slice_in_dim(x, start, width, axis=x.ndim - 1)


def reduce_half(x, bit, bits):
    w = x.shape[-1] // 2
    h = side(bit, bits)
    keep = cols(x, h * w, w)
    send = cols(x, (1 - h) * w, w)
    return keep + swap(send, bit, bits)


def gather_half(x, bit, bits):
    w = x.shape[-1]
    h = side(bit, bits)
    both = jnp.concatenate([x, swap(x, bit, bits), x], axis=-1)
    return cols(both, h * w, 2 * w)


def on_device(templates, leaf_inverse, v_basis, u_basis, coupling):
    bits = bit_axes()
    levels, pixels, rank = v_basis.shape
    width = templates.shape[1]
    c0 = jnp.dot(leaf_inverse, templates, preferred_element_type=F32)

    mine_c = coupling[:, 0]
    partial = [
        jnp.einsum(
            "lir,is->lrs", v_basis[s + 1:], u_basis[s], preferred_element_type=F32
        ).reshape(-1, rank)
        for s in range(levels - 1)
    ]
    w_own, theirs_c = [None] * levels, []
    for b in range(levels):
        c = mine_c[b]
        parts = list(partial[b:])
        parts.append(jnp.concatenate([c[:, :rank], c[:, rank:]], axis=0).astype(F32))
        got = swap(jnp.concatenate(parts, axis=0), b, bits)
        theirs = got[got.shape[0] - 2 * rank :]
        theirs_c.append(jnp.concatenate([theirs[:rank], theirs[rank:]], axis=1))
        at = 0
        for s in range(b, levels - 1):
            n = partial[s].shape[0]
            recv = got[at : at + n]
            at += n
            if s == b:
                w_own[s] = jnp.concatenate([partial[s], recv], axis=1)
            else:
                partial[s] = partial[s] + recv
    couple = []
    for s in range(levels):
        lower = side(s, bits) == 0
        mine, theirs = mine_c[s], theirs_c[s]
        first = jnp.concatenate([mine[:, :rank], theirs[:, :rank]], axis=0)
        second = jnp.concatenate([mine[:, rank:], theirs[:, rank:]], axis=0)
        couple.append(
            jnp.concatenate(
                [jnp.where(lower, first, second), jnp.where(lower, second, first)],
                axis=1,
            )
        )

    vl = jnp.einsum("lir,ij->lrj", v_basis, leaf_inverse, preferred_element_type=F32)
    vl_hi = vl.astype(BF16)
    vl_lo = (vl - vl_hi.astype(F32)).astype(BF16)

    def project(lv, x):
        return jnp.einsum(
            "lrj,jt->lrt", vl_hi[lv], x, preferred_element_type=F32
        ) + jnp.einsum("lrj,jt->lrt", vl_lo[lv], x, preferred_element_type=F32)

    proj0 = project(slice(0, 1), templates)[0]
    rest = None
    if levels > 1:
        half = width // 2
        h = side(0, bits)
        keep = project(slice(1, levels), cols(templates, h * half, half))
        send = project(slice(1, levels), cols(templates, (1 - h) * half, half))
        rest = keep + swap(send, 0, bits)
    own_coefs = []
    for s in range(levels):
        if s == 0:
            mine_b = proj0.astype(BF16)
            theirs_b = swap(mine_b, s, bits)
        else:
            mine_b = rest[0].astype(BF16)
            rest = rest[1:]
            n = rest.shape[0]
            w = mine_b.shape[1] // 2
            parts = [mine_b[:, :w], mine_b[:, w:]]
            summed = n == 1 and s == levels - 2
            if summed:
                last = rest[0].astype(BF16)
                parts += [last[:, :w], last[:, w:]]
            elif n > 0:
                h = side(s, bits)
                keep = cols(rest, h * w, w)
                send = cols(rest, (1 - h) * w, w)
                parts.append(send.astype(BF16).reshape(n * rank, w))
            got = swap(jnp.concatenate(parts, axis=0), s, bits)
            theirs_b = jnp.concatenate([got[:rank], got[rank : 2 * rank]], axis=1)
            if summed:
                recv = jnp.concatenate([got[2 * rank : 3 * rank], got[3 * rank :]], axis=1)
                rest = rest + recv.astype(F32)[None]
            elif n > 0:
                recv = got[2 * rank :].reshape(n, rank, w).astype(F32)
                rest = keep + recv
        stacked = jnp.concatenate([mine_b, theirs_b], axis=0)
        coefs = jnp.dot(couple[s], stacked, preferred_element_type=F32).astype(BF16)
        own_coefs.append(coefs[:rank])
        if s < levels - 1:
            w = coefs.shape[1] // 2
            if rest.shape[-1] == coefs.shape[1]:
                piece = coefs.astype(F32)
            else:
                piece = cols(coefs, side(s, bits) * w, w).astype(F32)
            fix = jnp.dot(
                w_own[s], piece, preferred_element_type=F32,
                precision=lax.Precision.HIGHEST,
            )
            rest = rest - fix.reshape(rest.shape)

    full = [own_coefs[0]] + [None] * (levels - 1)
    pending = {s: own_coefs[s] for s in range(1, levels)}
    top = {s: s - 1 for s in range(1, levels)}
    if levels > 2:
        top[levels - 1] = levels - 3
    for j in reversed(range(levels - 1)):
        group = [s for s in range(1, levels) if top[s] >= j]
        if not group:
            continue
        joined = gather_half(jnp.stack([pending[s] for s in group]), j, bits)
        for i, s in enumerate(group):
            pending[s] = joined[i]
    for s in range(1, levels):
        full[s] = pending[s]
    current = c0
    for s in range(levels):
        current = current - jnp.dot(u_basis[s], full[s], preferred_element_type=F32)
    return current.astype(BF16)


def solution(mesh):
    placed = (
        P(("slab", "wide", "narrow", "inner"), None),
        P(("slab", "wide", "narrow", "inner"), None),
        P(None, ("slab", "wide", "narrow", "inner"), None),
        P(None, ("slab", "wide", "narrow", "inner"), None),
        P(None, ("slab", "wide", "narrow", "inner"), None, None),
    )
    return jax.shard_map(
        on_device,
        mesh=mesh,
        in_specs=placed,
        out_specs=P(("slab", "wide", "narrow", "inner"), None),
        check_vma=False,
    )
```

```python
import jax
import jax.numpy as jnp
from jax import lax
from jax.sharding import PartitionSpec as P

F32 = jnp.float32
BF16 = jnp.bfloat16


def bit_axes():
    bits = []
    for axis in ("inner", "narrow", "wide"):
        for stride in range(lax.axis_size(axis).bit_length() - 1):
            bits.append((axis, stride))
    return bits


def swap(x, bit, bits):
    axis, stride = bits[bit]
    n = lax.axis_size(axis)
    return lax.ppermute(x, axis, [(i, i ^ (1 << stride)) for i in range(n)])


def side(bit, bits):
    axis, stride = bits[bit]
    return (lax.axis_index(axis) >> stride) & 1


def cols(x, start, width):
    return lax.dynamic_slice_in_dim(x, start, width, axis=x.ndim - 1)


def reduce_half(x, bit, bits):
    w = x.shape[-1] // 2
    h = side(bit, bits)
    keep = cols(x, h * w, w)
    send = cols(x, (1 - h) * w, w)
    return keep + swap(send, bit, bits)


def gather_half(x, bit, bits):
    w = x.shape[-1]
    h = side(bit, bits)
    both = jnp.concatenate([x, swap(x, bit, bits), x], axis=-1)
    return cols(both, h * w, 2 * w)


def on_device(templates, leaf_inverse, v_basis, u_basis, coupling):
    bits = bit_axes()
    levels, pixels, rank = v_basis.shape
    width = templates.shape[1]
    c0 = jnp.dot(leaf_inverse, templates, preferred_element_type=F32)

    mine_c = coupling[:, 0]
    partial = [
        jnp.einsum(
            "lir,is->lrs", v_basis[s + 1:], u_basis[s], preferred_element_type=F32
        ).reshape(-1, rank)
        for s in range(levels - 1)
    ]
    w_own, theirs_c = [None] * levels, []
    for b in range(levels):
        c = mine_c[b]
        parts = [jnp.concatenate([c[:, :rank], c[:, rank:]], axis=0).astype(F32)]
        parts += partial[b:]
        got = swap(jnp.concatenate(parts, axis=0), b, bits)
        theirs = got[: 2 * rank]
        theirs_c.append(jnp.concatenate([theirs[:rank], theirs[rank:]], axis=1))
        if b < levels - 1:
            n = partial[b].shape[0]
            w_own[b] = jnp.concatenate(
                [partial[b], got[2 * rank : 2 * rank + n]], axis=1
            )
            if b + 1 < levels - 1:
                later = jnp.concatenate(partial[b + 1 :], axis=0)
                later = later + got[2 * rank + n :]
                at = 0
                for s in range(b + 1, levels - 1):
                    k = partial[s].shape[0]
                    partial[s] = later[at : at + k]
                    at += k
    couple = []
    for s in range(levels):
        lower = side(s, bits) == 0
        mine, theirs = mine_c[s], theirs_c[s]
        first = jnp.concatenate([mine[:, :rank], theirs[:, :rank]], axis=0)
        second = jnp.concatenate([mine[:, rank:], theirs[:, rank:]], axis=0)
        couple.append(
            jnp.concatenate(
                [jnp.where(lower, first, second), jnp.where(lower, second, first)],
                axis=1,
            )
        )

    vl = jnp.einsum("lir,ij->lrj", v_basis, leaf_inverse, preferred_element_type=F32)
    vl_hi = vl.astype(BF16)
    vl_lo = (vl - vl_hi.astype(F32)).astype(BF16)

    def project(lv, x):
        return jnp.einsum(
            "lrj,jt->lrt", vl_hi[lv], x, preferred_element_type=F32
        ) + jnp.einsum("lrj,jt->lrt", vl_lo[lv], x, preferred_element_type=F32)

    proj0 = project(slice(0, 1), templates)[0]
    rest = None
    if levels > 1:
        half = width // 2
        h = side(0, bits)
        keep = project(slice(1, levels), cols(templates, h * half, half))
        send = project(slice(1, levels), cols(templates, (1 - h) * half, half))
        rest = keep + swap(send, 0, bits)
    own_coefs = []
    for s in range(levels):
        if s == 0:
            mine_b = proj0.astype(BF16)
            theirs_b = swap(mine_b, s, bits)
        else:
            mine_b = rest[0].astype(BF16)
            rest = rest[1:]
            n = rest.shape[0]
            w = mine_b.shape[1] // 2
            parts = [mine_b[:, :w], mine_b[:, w:]]
            summed = n == 1 and s == levels - 2
            if summed:
                last = rest[0].astype(BF16)
                parts += [last[:, :w], last[:, w:]]
            elif n > 0:
                h = side(s, bits)
                keep = cols(rest, h * w, w)
                send = cols(rest, (1 - h) * w, w)
                parts.append(send.astype(BF16).reshape(n * rank, w))
            got = swap(jnp.concatenate(parts, axis=0), s, bits)
            theirs_b = jnp.concatenate([got[:rank], got[rank : 2 * rank]], axis=1)
            if summed:
                recv = jnp.concatenate([got[2 * rank : 3 * rank], got[3 * rank :]], axis=1)
                rest = rest + recv.astype(F32)[None]
            elif n > 0:
                recv = got[2 * rank :].reshape(n, rank, w).astype(F32)
                rest = keep + recv
        stacked = jnp.concatenate([mine_b, theirs_b], axis=0)
        coefs = jnp.dot(couple[s], stacked, preferred_element_type=F32).astype(BF16)
        own_coefs.append(coefs[:rank])
        if s < levels - 1:
            w = coefs.shape[1] // 2
            if rest.shape[-1] == coefs.shape[1]:
                piece = coefs.astype(F32)
            else:
                piece = cols(coefs, side(s, bits) * w, w).astype(F32)
            fix = jnp.dot(
                w_own[s], piece, preferred_element_type=F32,
                precision=lax.Precision.HIGHEST,
            )
            rest = rest - fix.reshape(rest.shape)

    full = [own_coefs[0]] + [None] * (levels - 1)
    pending = {s: own_coefs[s] for s in range(1, levels)}
    top = {s: s - 1 for s in range(1, levels)}
    if levels > 2:
        top[levels - 1] = levels - 3
    for j in reversed(range(levels - 1)):
        group = [s for s in range(1, levels) if top[s] >= j]
        if not group:
            continue
        joined = gather_half(jnp.stack([pending[s] for s in group]), j, bits)
        for i, s in enumerate(group):
            pending[s] = joined[i]
    for s in range(1, levels):
        full[s] = pending[s]
    current = c0
    for s in range(levels):
        current = current - jnp.dot(u_basis[s], full[s], preferred_element_type=F32)
    return current.astype(BF16)


def solution(mesh):
    placed = (
        P(("slab", "wide", "narrow", "inner"), None),
        P(("slab", "wide", "narrow", "inner"), None),
        P(None, ("slab", "wide", "narrow", "inner"), None),
        P(None, ("slab", "wide", "narrow", "inner"), None),
        P(None, ("slab", "wide", "narrow", "inner"), None, None),
    )
    return jax.shard_map(
        on_device,
        mesh=mesh,
        in_specs=placed,
        out_specs=P(("slab", "wide", "narrow", "inner"), None),
        check_vma=False,
    )
```

```python
import jax
import jax.numpy as jnp
from jax import lax
from jax.sharding import PartitionSpec as P

F32 = jnp.float32
BF16 = jnp.bfloat16


def bit_axes():
    bits = []
    for axis in ("inner", "narrow", "wide"):
        for stride in range(lax.axis_size(axis).bit_length() - 1):
            bits.append((axis, stride))
    return bits


def swap(x, bit, bits):
    axis, stride = bits[bit]
    n = lax.axis_size(axis)
    return lax.ppermute(x, axis, [(i, i ^ (1 << stride)) for i in range(n)])


def side(bit, bits):
    axis, stride = bits[bit]
    return (lax.axis_index(axis) >> stride) & 1


def cols(x, start, width):
    return lax.dynamic_slice_in_dim(x, start, width, axis=x.ndim - 1)


def reduce_half(x, bit, bits):
    w = x.shape[-1] // 2
    h = side(bit, bits)
    keep = cols(x, h * w, w)
    send = cols(x, (1 - h) * w, w)
    return keep + swap(send, bit, bits)


def gather_half(x, bit, bits):
    w = x.shape[-1]
    h = side(bit, bits)
    both = jnp.concatenate([x, swap(x, bit, bits), x], axis=-1)
    return cols(both, h * w, 2 * w)


def on_device(templates, leaf_inverse, v_basis, u_basis, coupling):
    bits = bit_axes()
    levels, pixels, rank = v_basis.shape
    width = templates.shape[1]
    c0 = jnp.dot(leaf_inverse, templates, preferred_element_type=F32)

    mine_c = coupling[:, 0]
    partial = [
        jnp.einsum(
            "lir,is->lrs", v_basis[s + 1:], u_basis[s], preferred_element_type=F32
        ).reshape(-1, rank)
        for s in range(levels - 1)
    ]
    w_own, theirs_c = [None] * levels, []
    for b in range(levels):
        c = mine_c[b]
        parts = list(partial[b:])
        parts.append(jnp.concatenate([c[:, :rank], c[:, rank:]], axis=0).astype(F32))
        got = swap(jnp.concatenate(parts, axis=0), b, bits)
        theirs = got[got.shape[0] - 2 * rank :]
        got = got[: got.shape[0] - 2 * rank]
        theirs_c.append(jnp.concatenate([theirs[:rank], theirs[rank:]], axis=1))
        if b < levels - 1:
            n = partial[b].shape[0]
            w_own[b] = jnp.concatenate(
                [partial[b], got[:n]], axis=1
            )
            if b + 1 < levels - 1:
                later = jnp.concatenate(partial[b + 1 :], axis=0)
                later = later + got[n:]
                at = 0
                for s in range(b + 1, levels - 1):
                    k = partial[s].shape[0]
                    partial[s] = later[at : at + k]
                    at += k
    couple = []
    for s in range(levels):
        lower = side(s, bits) == 0
        mine, theirs = mine_c[s], theirs_c[s]
        first = jnp.concatenate([mine[:, :rank], theirs[:, :rank]], axis=0)
        second = jnp.concatenate([mine[:, rank:], theirs[:, rank:]], axis=0)
        couple.append(
            jnp.concatenate(
                [jnp.where(lower, first, second), jnp.where(lower, second, first)],
                axis=1,
            )
        )

    vl = jnp.einsum("lir,ij->lrj", v_basis, leaf_inverse, preferred_element_type=F32)
    vl_hi = vl.astype(BF16)
    vl_lo = (vl - vl_hi.astype(F32)).astype(BF16)

    def project(lv, x):
        return jnp.einsum(
            "lrj,jt->lrt", vl_hi[lv], x, preferred_element_type=F32
        ) + jnp.einsum("lrj,jt->lrt", vl_lo[lv], x, preferred_element_type=F32)

    proj0 = project(slice(0, 1), templates)[0]
    rest = None
    if levels > 1:
        half = width // 2
        h = side(0, bits)
        keep = project(slice(1, levels), cols(templates, h * half, half))
        send = project(slice(1, levels), cols(templates, (1 - h) * half, half))
        rest = keep + swap(send, 0, bits)
    own_coefs = []
    for s in range(levels):
        if s == 0:
            mine_b = proj0.astype(BF16)
            theirs_b = swap(mine_b, s, bits)
        else:
            mine_b = rest[0].astype(BF16)
            rest = rest[1:]
            n = rest.shape[0]
            w = mine_b.shape[1] // 2
            parts = [mine_b[:, :w], mine_b[:, w:]]
            summed = n == 1 and s == levels - 2
            if summed:
                last = rest[0].astype(BF16)
                parts += [last[:, :w], last[:, w:]]
            elif n > 0:
                h = side(s, bits)
                keep = cols(rest, h * w, w)
                send = cols(rest, (1 - h) * w, w)
                parts.append(send.astype(BF16).reshape(n * rank, w))
            got = swap(jnp.concatenate(parts, axis=0), s, bits)
            theirs_b = jnp.concatenate([got[:rank], got[rank : 2 * rank]], axis=1)
            if summed:
                recv = jnp.concatenate([got[2 * rank : 3 * rank], got[3 * rank :]], axis=1)
                rest = rest + recv.astype(F32)[None]
            elif n > 0:
                recv = got[2 * rank :].reshape(n, rank, w).astype(F32)
                rest = keep + recv
        stacked = jnp.concatenate([mine_b, theirs_b], axis=0)
        coefs = jnp.dot(couple[s], stacked, preferred_element_type=F32).astype(BF16)
        own_coefs.append(coefs[:rank])
        if s < levels - 1:
            w = coefs.shape[1] // 2
            if rest.shape[-1] == coefs.shape[1]:
                piece = coefs.astype(F32)
            else:
                piece = cols(coefs, side(s, bits) * w, w).astype(F32)
            fix = jnp.dot(
                w_own[s], piece, preferred_element_type=F32,
                precision=lax.Precision.HIGHEST,
            )
            rest = rest - fix.reshape(rest.shape)

    full = [own_coefs[0]] + [None] * (levels - 1)
    pending = {s: own_coefs[s] for s in range(1, levels)}
    top = {s: s - 1 for s in range(1, levels)}
    if levels > 2:
        top[levels - 1] = levels - 3
    for j in reversed(range(levels - 1)):
        group = [s for s in range(1, levels) if top[s] >= j]
        if not group:
            continue
        joined = gather_half(jnp.stack([pending[s] for s in group]), j, bits)
        for i, s in enumerate(group):
            pending[s] = joined[i]
    for s in range(1, levels):
        full[s] = pending[s]
    current = c0
    for s in range(levels):
        current = current - jnp.dot(u_basis[s], full[s], preferred_element_type=F32)
    return current.astype(BF16)


def solution(mesh):
    placed = (
        P(("slab", "wide", "narrow", "inner"), None),
        P(("slab", "wide", "narrow", "inner"), None),
        P(None, ("slab", "wide", "narrow", "inner"), None),
        P(None, ("slab", "wide", "narrow", "inner"), None),
        P(None, ("slab", "wide", "narrow", "inner"), None, None),
    )
    return jax.shard_map(
        on_device,
        mesh=mesh,
        in_specs=placed,
        out_specs=P(("slab", "wide", "narrow", "inner"), None),
        check_vma=False,
    )
```

```python
import jax
import jax.numpy as jnp
from jax import lax
from jax.sharding import PartitionSpec as P

F32 = jnp.float32
BF16 = jnp.bfloat16


def bit_axes():
    bits = []
    for axis in ("inner", "narrow", "wide"):
        for stride in range(lax.axis_size(axis).bit_length() - 1):
            bits.append((axis, stride))
    return bits


def swap(x, bit, bits):
    axis, stride = bits[bit]
    n = lax.axis_size(axis)
    return lax.ppermute(x, axis, [(i, i ^ (1 << stride)) for i in range(n)])


def side(bit, bits):
    axis, stride = bits[bit]
    return (lax.axis_index(axis) >> stride) & 1


def cols(x, start, width):
    return lax.dynamic_slice_in_dim(x, start, width, axis=x.ndim - 1)


def reduce_half(x, bit, bits):
    w = x.shape[-1] // 2
    h = side(bit, bits)
    keep = cols(x, h * w, w)
    send = cols(x, (1 - h) * w, w)
    return keep + swap(send, bit, bits)


def gather_half(x, bit, bits):
    w = x.shape[-1]
    h = side(bit, bits)
    both = jnp.concatenate([x, swap(x, bit, bits), x], axis=-1)
    return cols(both, h * w, 2 * w)


def on_device(templates, leaf_inverse, v_basis, u_basis, coupling):
    bits = bit_axes()
    levels, pixels, rank = v_basis.shape
    width = templates.shape[1]
    c0 = jnp.dot(leaf_inverse, templates, preferred_element_type=F32)

    mine_c = coupling[:, 0]
    partial = [
        jnp.einsum(
            "lir,is->lrs", v_basis[s + 1:], u_basis[s], preferred_element_type=F32
        ).reshape(-1, rank)
        for s in range(levels - 1)
    ]
    w_own, theirs_c = [None] * levels, []
    for b in range(levels):
        c = mine_c[b]
        parts = [jnp.concatenate([c[:, :rank], c[:, rank:]], axis=0).astype(F32)]
        parts += partial[b:]
        got = swap(jnp.concatenate(parts, axis=0), b, bits)
        theirs = got[: 2 * rank]
        theirs_c.append(jnp.concatenate([theirs[:rank], theirs[rank:]], axis=1))
        if b < levels - 1:
            n = partial[b].shape[0]
            w_own[b] = jnp.concatenate(
                [partial[b], got[2 * rank : 2 * rank + n]], axis=1
            )
            if b + 1 < levels - 1:
                later = jnp.concatenate(partial[b + 1 :], axis=0)
                later = later + got[2 * rank + n :]
                at = 0
                for s in range(b + 1, levels - 1):
                    k = partial[s].shape[0]
                    partial[s] = later[at : at + k]
                    at += k
    couple = []
    for s in range(levels):
        lower = side(s, bits) == 0
        mine, theirs = mine_c[s], theirs_c[s]
        first = jnp.concatenate([mine[:, :rank], theirs[:, :rank]], axis=0)
        second = jnp.concatenate([mine[:, rank:], theirs[:, rank:]], axis=0)
        couple.append(
            jnp.concatenate(
                [jnp.where(lower, first, second), jnp.where(lower, second, first)],
                axis=1,
            )
        )

    vl = jnp.einsum("lir,ij->lrj", v_basis, leaf_inverse, preferred_element_type=F32)
    vl_hi = vl.astype(BF16)
    vl_lo = (vl - vl_hi.astype(F32)).astype(BF16)

    def project(lv, x):
        return jnp.einsum(
            "lrj,jt->lrt", vl_hi[lv], x, preferred_element_type=F32
        ) + jnp.einsum("lrj,jt->lrt", vl_lo[lv], x, preferred_element_type=F32)

    proj0 = project(slice(0, 1), templates)[0]
    rest = None
    if levels > 1:
        half = width // 2
        h = side(0, bits)
        keep = project(slice(1, levels), cols(templates, h * half, half))
        send = project(slice(1, levels), cols(templates, (1 - h) * half, half))
        rest = keep + swap(send, 0, bits)
    own_coefs = []
    for s in range(levels):
        if s == 0:
            mine_b = proj0.astype(BF16)
            theirs_b = swap(mine_b, s, bits)
        else:
            mine_b = rest[0].astype(BF16)
            rest = rest[1:]
            n = rest.shape[0]
            w = mine_b.shape[1] // 2
            parts = [mine_b[:, :w], mine_b[:, w:]]
            summed = n == 1 and s == levels - 2
            if summed:
                last = rest[0].astype(BF16)
                parts += [last[:, :w], last[:, w:]]
            elif n > 0:
                h = side(s, bits)
                keep = cols(rest, h * w, w)
                send = cols(rest, (1 - h) * w, w)
                parts.append(send.astype(BF16).reshape(n * rank, w))
            got = swap(jnp.concatenate(parts, axis=0), s, bits)
            theirs_b = jnp.concatenate([got[:rank], got[rank : 2 * rank]], axis=1)
            if summed:
                recv = jnp.concatenate([got[2 * rank : 3 * rank], got[3 * rank :]], axis=1)
                rest = rest + recv.astype(F32)[None]
            elif n > 0:
                recv = got[2 * rank :].reshape(n, rank, w).astype(F32)
                rest = keep + recv
        stacked = jnp.concatenate([mine_b, theirs_b], axis=0)
        rows = couple[s] if s < levels - 1 else couple[s][:rank]
        coefs = jnp.dot(rows, stacked, preferred_element_type=F32).astype(BF16)
        own_coefs.append(coefs[:rank])
        if s < levels - 1:
            w = coefs.shape[1] // 2
            if rest.shape[-1] == coefs.shape[1]:
                piece = coefs.astype(F32)
            else:
                piece = cols(coefs, side(s, bits) * w, w).astype(F32)
            fix = jnp.dot(
                w_own[s], piece, preferred_element_type=F32,
                precision=lax.Precision.HIGHEST,
            )
            rest = rest - fix.reshape(rest.shape)

    full = [own_coefs[0]] + [None] * (levels - 1)
    pending = {s: own_coefs[s] for s in range(1, levels)}
    top = {s: s - 1 for s in range(1, levels)}
    if levels > 2:
        top[levels - 1] = levels - 3
    for j in reversed(range(levels - 1)):
        group = [s for s in range(1, levels) if top[s] >= j]
        if not group:
            continue
        joined = gather_half(jnp.stack([pending[s] for s in group]), j, bits)
        for i, s in enumerate(group):
            pending[s] = joined[i]
    for s in range(1, levels):
        full[s] = pending[s]
    current = c0
    for s in range(levels):
        current = current - jnp.dot(u_basis[s], full[s], preferred_element_type=F32)
    return current.astype(BF16)


def solution(mesh):
    placed = (
        P(("slab", "wide", "narrow", "inner"), None),
        P(("slab", "wide", "narrow", "inner"), None),
        P(None, ("slab", "wide", "narrow", "inner"), None),
        P(None, ("slab", "wide", "narrow", "inner"), None),
        P(None, ("slab", "wide", "narrow", "inner"), None, None),
    )
    return jax.shard_map(
        on_device,
        mesh=mesh,
        in_specs=placed,
        out_specs=P(("slab", "wide", "narrow", "inner"), None),
        check_vma=False,
    )
```
